32 devices in a mesh: row: 4 (over z), col: 8 (over y, x, core).
Axes of the slice: x: 2, y: 2, z: 4, core: 2. Of those that a mesh axis runs over, the one named last changes fastest.
Arguments:
- image: float32 [224, 32, 2048], P(None, 'row', 'col'), may hold values from -24 to 24
- start_basis: float32 [224, 16], replicated, may hold values from -4 to 4
Outputs:
- smoothed: float32 [224, 32, 2048], P(None, 'row', 'col')
- lowrank: float32 [224, 32, 2048], P(None, 'row', 'col')
The draws below stay inside these ranges and needn't reach their ends.
All inputs are finite; a program needn't handle non-finite values.
Results may differ from the reference program's by a relative error of at most 0.0003.
Values sent between devices are 32-bit elements; how exact they have to be, the bound alone decides.
No kernel may reach another device: no remote copies, remote signals or barrier semaphores. Data moves between devices by JAX's collectives and lax.ppermute only.
A program may use at most 64 MiB of HBM per device.

```python
import math
import jax
import jax.numpy as jnp
from jax import lax

BANDS = 224
RANK = 16
SWEEPS = 4
SUBIT = 2
HEIGHT = 32
WIDTH = 2048


def draw_image(key, part):
    keys = jax.random.split(key, 2)
    band_scale = jnp.exp(jax.random.uniform(keys[0], (BANDS, 1, 1), jnp.float32, math.log(0.5), math.log(2.0)))
    row_ramp = 3.0 ** (jnp.arange(HEIGHT, dtype=jnp.float32) / max(HEIGHT - 1, 1))
    col_ramp = 3.0 ** (jnp.arange(WIDTH, dtype=jnp.float32) / max(WIDTH - 1, 1))
    scale_all = 0.25 * band_scale * row_ramp[None, :, None] * col_ramp[None, None, :]
    base_vals = jnp.clip(jax.random.normal(keys[1], (BANDS, HEIGHT, WIDTH), jnp.float32), -4.0, 4.0)
    return (scale_all * base_vals).astype(jnp.float32)


def gaussian(key, extent, width, reach, kind=jnp.bfloat16):
    return jnp.clip(width * jax.random.normal(key, extent, jnp.float32), -reach, reach).astype(kind)


def setup_inputs(seed: int = 0) -> dict:
    key_list = jax.random.split(jax.random.key(seed), 3)
    return {
        "image": draw_image(jax.random.fold_in(key_list[2], 71), 0),
        "start_basis": gaussian(key_list[1], (BANDS, RANK), 1.0, 4.0, jnp.float32),
    }


tau_step = 0.22
fidelity = 0.1

def forward_diffs(padded):
    diff_col = padded[..., :-1, 1:] - padded[..., :-1, :-1]
    diff_row = padded[..., 1:, :-1] - padded[..., :-1, :-1]
    return (diff_col, diff_row)

def relax_cells(padded, diff_col, diff_row, source, weight):
    flux_col = weight * diff_col
    flux_row = weight * diff_row
    spread = flux_col[..., 1:, 1:] - flux_col[..., 1:, :-1] + flux_row[..., 1:, 1:] - flux_row[..., :-1, 1:]
    centre = padded[..., 1:-1, 1:-1]
    return centre + tau_step * spread + tau_step * fidelity * (source - centre)

def orthonormal(block):
    inner = jnp.dot(block.T, block, precision=lax.Precision.HIGHEST)
    lower = jnp.linalg.cholesky(inner)
    return lax.linalg.triangular_solve(lower, block, left_side=False, lower=True, transpose_a=True)

def subspace_basis(gram_full, start_basis):
    basis_now = start_basis
    for turn in range(SUBIT):
        product = jnp.dot(gram_full, basis_now, precision=lax.Precision.HIGHEST)
        basis_now = orthonormal(orthonormal(product))
    return basis_now

def reference(image, start_basis):
    field = image
    groups = BANDS // 8
    source_blocks = image.reshape(groups, 8, HEIGHT, WIDTH)
    for sweep_no in range(SWEEPS):
        padded = jnp.pad(field, ((0, 0), (1, 1), (1, 1)))
        blocks = padded.reshape(groups, 8, HEIGHT + 2, WIDTH + 2)

        def accumulate(energy_sum, block):
            diff_col, diff_row = forward_diffs(block)
            return (energy_sum + lax.optimization_barrier(jnp.sum(diff_col * diff_col + diff_row * diff_row, axis=0)), None)
        energy_sum, unused = lax.scan(accumulate, jnp.zeros((HEIGHT + 1, WIDTH + 1), jnp.float32), blocks)
        weight = 1.0 / jnp.sqrt(1.0 + energy_sum / BANDS)

        def relax_block(pair):
            diff_col, diff_row = forward_diffs(pair[0])
            return relax_cells(pair[0], diff_col, diff_row, pair[1], weight)
        field = lax.map(relax_block, (blocks, source_blocks)).reshape(BANDS, HEIGHT, WIDTH)
    flat_field = field.reshape(BANDS, HEIGHT * WIDTH)
    gram_full = lax.dot_general(flat_field.astype(jnp.float32), flat_field.astype(jnp.float32), (((1,), (1,)), ((), ())), precision=lax.Precision.HIGHEST, preferred_element_type=jnp.float32)
    basis_now = subspace_basis(gram_full, start_basis)
    coeffs = jnp.dot(basis_now.T, flat_field, precision=lax.Precision.HIGHEST)
    lowrank = jnp.dot(basis_now, coeffs, precision=lax.Precision.HIGHEST)
    return (field, lowrank.reshape(BANDS, HEIGHT, WIDTH))
```

```python
import jax
import jax.numpy as jnp
from jax import lax
from jax.sharding import PartitionSpec as P

SWEEPS = 4
SUBIT = 2


tau_step = 0.22
fidelity = 0.1


def padded_2(cells, sides, width):
    for axis, dim in sides:
        count = lax.axis_size(axis)
        ends = count - 1
        head = lax.slice_in_dim(cells, 0, width, axis=dim)
        tail = lax.slice_in_dim(cells, cells.shape[dim] - width, cells.shape[dim], axis=dim)
        cells = jnp.concatenate(
            [
                lax.ppermute(tail, axis, [(i, (i + 1) % count) for i in range(ends)]),
                cells,
                lax.ppermute(head, axis, [((i + 1) % count, i) for i in range(ends)]),
            ],
            axis=dim,
        )
    return cells


def forward_diffs(padded):
    diff_col = padded[..., :-1, 1:] - padded[..., :-1, :-1]
    diff_row = padded[..., 1:, :-1] - padded[..., :-1, :-1]
    return (diff_col, diff_row)


def smooth_step(padded, source):
    diff_col, diff_row = forward_diffs(padded)
    energy_sum = jnp.sum(diff_col * diff_col + diff_row * diff_row, axis=0)
    weight = 1.0 / jnp.sqrt(1.0 + energy_sum / padded.shape[0])
    flux_col = weight * diff_col
    flux_row = weight * diff_row
    spread = (
        flux_col[..., 1:, 1:]
        - flux_col[..., 1:, :-1]
        + flux_row[..., 1:, 1:]
        - flux_row[..., :-1, 1:]
    )
    centre = padded[..., 1:-1, 1:-1]
    return centre + tau_step * spread + tau_step * fidelity * (source - centre)


def butterfly_sum(value, axes):
    for axis in axes:
        count = lax.axis_size(axis)
        if count & (count - 1):
            value = lax.psum(value, axis)
            continue
        step = 1
        while step < count:
            partner = lax.ppermute(value, axis, [(i, i ^ step) for i in range(count)])
            value = value + partner
            step *= 2
    return value


def orthonormal(block):
    inner = jnp.dot(block.T, block, precision=lax.Precision.HIGHEST)
    lower = jnp.linalg.cholesky(inner)
    return lax.linalg.triangular_solve(lower, block, left_side=False, lower=True, transpose_a=True)


def shards(image, start_basis):
    band_count, tile_rows, tile_cols = image.shape
    field = image
    for sweep_no in range(SWEEPS):
        extended = padded_2(field, (("row", 1), ("col", 2)), 1)
        field = smooth_step(extended, image)
    flat_field = field.reshape(band_count, tile_rows * tile_cols)
    basis_now = start_basis
    local_gram = lax.dot_general(
        flat_field,
        flat_field,
        (((1,), (1,)), ((), ())),
        precision=lax.Precision.HIGHEST,
        preferred_element_type=jnp.float32,
    )
    gram_full = butterfly_sum(local_gram, ("col", "row"))
    for turn in range(SUBIT):
        product = jnp.dot(gram_full, basis_now, precision=lax.Precision.HIGHEST)
        basis_now = orthonormal(orthonormal(product))
    coeffs = jnp.dot(basis_now.T, flat_field, precision=lax.Precision.HIGHEST)
    lowrank = jnp.dot(basis_now, coeffs, precision=lax.Precision.HIGHEST)
    return (field, lowrank.reshape(band_count, tile_rows, tile_cols))


def solution(mesh):
    in_specs = (P(None, "row", "col"), P())
    out_specs = (P(None, "row", "col"), P(None, "row", "col"))
    return jax.shard_map(shards, mesh=mesh, in_specs=in_specs, out_specs=out_specs, check_vma=False)
```

```python
import jax
import jax.numpy as jnp
from jax import lax
from jax.sharding import PartitionSpec as P

SWEEPS = 4
SUBIT = 2


tau_step = 0.22
fidelity = 0.1


def butterfly_sum(value, axes):
    for axis in axes:
        count = lax.axis_size(axis)
        if count & (count - 1):
            value = lax.psum(value, axis)
            continue
        step = 1
        while step < count:
            partner = lax.ppermute(value, axis, [(i, i ^ step) for i in range(count)])
            value = value + partner
            step *= 2
    return value


def with_halo(cells, axis, dim, width):
    count = lax.axis_size(axis)
    size = cells.shape[dim]
    head = lax.slice_in_dim(cells, 0, width, axis=dim)
    tail = lax.slice_in_dim(cells, size - width, size, axis=dim)
    before = lax.ppermute(tail, axis, [(i, i + 1) for i in range(count - 1)])
    after = lax.ppermute(head, axis, [(i + 1, i) for i in range(count - 1)])
    return jnp.concatenate([before, cells, after], axis=dim)


def inside_mask(axis, tile, width):
    count = lax.axis_size(axis)
    start = lax.axis_index(axis) * tile - width
    index = start + jnp.arange(tile + 2 * width, dtype=jnp.int32)
    return (index >= 0) & (index < count * tile)


def sweep(field, source, keep):
    diff_col = field[:-1, 1:] - field[:-1, :-1]
    diff_row = field[1:, :-1] - field[:-1, :-1]
    energy_sum = jnp.sum(diff_col * diff_col + diff_row * diff_row, axis=-1, keepdims=True)
    weight = 1.0 / jnp.sqrt(1.0 + energy_sum / field.shape[-1])
    flux_col = weight * diff_col
    flux_row = weight * diff_row
    spread = flux_col[1:, 1:] - flux_col[1:, :-1] + flux_row[1:, 1:] - flux_row[:-1, 1:]
    centre = field[1:-1, 1:-1]
    new = centre + tau_step * spread + tau_step * fidelity * (source - centre)
    return jnp.where(keep, new, 0.0)


def orthonormal(block):
    inner = jnp.dot(block.T, block, precision=lax.Precision.HIGHEST)
    lower = jnp.linalg.cholesky(inner)
    return lax.linalg.triangular_solve(lower, block, left_side=False, lower=True, transpose_a=True)


def shards(image, start_basis):
    band_count, tile_rows, tile_cols = image.shape
    width = SWEEPS
    cells = jnp.transpose(image, (1, 2, 0))
    ext = with_halo(cells, "row", 0, width)
    ext = with_halo(ext, "col", 1, width)
    row_in = inside_mask("row", tile_rows, width)
    col_in = inside_mask("col", tile_cols, width)
    field = ext
    for sweep_no in range(SWEEPS):
        left = width - sweep_no - 1
        lo = sweep_no + 1
        nr = tile_rows + 2 * left
        nc = tile_cols + 2 * left
        source = ext[lo:lo + nr, lo:lo + nc]
        keep = (row_in[lo:lo + nr, None] & col_in[None, lo:lo + nc])[:, :, None]
        field = sweep(field, source, keep)
    flat_cells = field.reshape(tile_rows * tile_cols, band_count)
    smoothed = jnp.transpose(field, (2, 0, 1))
    local_gram = lax.dot_general(
        flat_cells,
        flat_cells,
        (((0,), (0,)), ((), ())),
        precision=lax.Precision.HIGHEST,
        preferred_element_type=jnp.float32,
    )
    gram_full = butterfly_sum(local_gram, ("col", "row"))
    basis_now = start_basis
    for turn in range(SUBIT):
        product = jnp.dot(gram_full, basis_now, precision=lax.Precision.HIGHEST)
        basis_now = orthonormal(orthonormal(product))
    coeffs = jnp.dot(flat_cells, basis_now, precision=lax.Precision.HIGHEST)
    lowrank = lax.dot_general(
        basis_now,
        coeffs,
        (((1,), (1,)), ((), ())),
        precision=lax.Precision.HIGHEST,
    )
    return (smoothed, lowrank.reshape(band_count, tile_rows, tile_cols))


def solution(mesh):
    in_specs = (P(None, "row", "col"), P())
    out_specs = (P(None, "row", "col"), P(None, "row", "col"))
    return jax.shard_map(shards, mesh=mesh, in_specs=in_specs, out_specs=out_specs, check_vma=False)
```

```python
import jax
import jax.numpy as jnp
from jax import lax
from jax.sharding import PartitionSpec as P

SWEEPS = 4
SUBIT = 2


tau_step = 0.22
fidelity = 0.1


def butterfly_sum(value, axes):
    for axis in axes:
        count = lax.axis_size(axis)
        if count & (count - 1):
            value = lax.psum(value, axis)
            continue
        step = 1
        while step < count:
            partner = lax.ppermute(value, axis, [(i, i ^ step) for i in range(count)])
            value = value + partner
            step *= 2
    return value


def with_halo(cells, axis, dim, width):
    count = lax.axis_size(axis)
    size = cells.shape[dim]
    head = lax.slice_in_dim(cells, 0, width, axis=dim)
    tail = lax.slice_in_dim(cells, size - width, size, axis=dim)
    before = lax.ppermute(tail, axis, [(i, i + 1) for i in range(count - 1)])
    after = lax.ppermute(head, axis, [(i + 1, i) for i in range(count - 1)])
    return jnp.concatenate([before, cells, after], axis=dim)


def inside_mask(axis, tile, width):
    count = lax.axis_size(axis)
    start = lax.axis_index(axis) * tile - width
    index = start + jnp.arange(tile + 2 * width, dtype=jnp.int32)
    return (index >= 0) & (index < count * tile)


def sweep(field, source, keep):
    diff_col = field[:-1, 1:] - field[:-1, :-1]
    diff_row = field[1:, :-1] - field[:-1, :-1]
    energy_sum = jnp.sum(diff_col * diff_col + diff_row * diff_row, axis=-1, keepdims=True)
    weight = 1.0 / jnp.sqrt(1.0 + energy_sum / field.shape[-1])
    flux_col = weight * diff_col
    flux_row = weight * diff_row
    spread = flux_col[1:, 1:] - flux_col[1:, :-1] + flux_row[1:, 1:] - flux_row[:-1, 1:]
    centre = field[1:-1, 1:-1]
    new = centre + tau_step * spread + tau_step * fidelity * (source - centre)
    return jnp.where(keep, new, 0.0)


def gram_times(flat_cells, basis):
    along = jnp.dot(flat_cells, basis, precision=lax.Precision.HIGHEST)
    return lax.dot_general(
        flat_cells,
        along,
        (((0,), (0,)), ((), ())),
        precision=lax.Precision.HIGHEST,
        preferred_element_type=jnp.float32,
    )


def orthonormal(block):
    inner = jnp.dot(block.T, block, precision=lax.Precision.HIGHEST)
    lower = jnp.linalg.cholesky(inner)
    return lax.linalg.triangular_solve(lower, block, left_side=False, lower=True, transpose_a=True)


def shards(image, start_basis):
    band_count, tile_rows, tile_cols = image.shape
    width = SWEEPS
    cells = jnp.transpose(image, (1, 2, 0))
    ext = with_halo(cells, "row", 0, width)
    ext = with_halo(ext, "col", 1, width)
    row_in = inside_mask("row", tile_rows, width)
    col_in = inside_mask("col", tile_cols, width)
    field = ext
    for sweep_no in range(SWEEPS):
        left = width - sweep_no - 1
        lo = sweep_no + 1
        nr = tile_rows + 2 * left
        nc = tile_cols + 2 * left
        source = ext[lo:lo + nr, lo:lo + nc]
        keep = (row_in[lo:lo + nr, None] & col_in[None, lo:lo + nc])[:, :, None]
        field = sweep(field, source, keep)
    flat_cells = field.reshape(tile_rows * tile_cols, band_count)
    smoothed = jnp.transpose(field, (2, 0, 1))
    basis_now = start_basis
    for turn in range(SUBIT):
        local_product = gram_times(flat_cells, basis_now)
        product = butterfly_sum(local_product, ("col", "row"))
        basis_now = orthonormal(orthonormal(product))
    coeffs = jnp.dot(flat_cells, basis_now, precision=lax.Precision.HIGHEST)
    lowrank = lax.dot_general(
        basis_now,
        coeffs,
        (((1,), (1,)), ((), ())),
        precision=lax.Precision.HIGHEST,
    )
    return (smoothed, lowrank.reshape(band_count, tile_rows, tile_cols))


def solution(mesh):
    in_specs = (P(None, "row", "col"), P())
    out_specs = (P(None, "row", "col"), P(None, "row", "col"))
    return jax.shard_map(shards, mesh=mesh, in_specs=in_specs, out_specs=out_specs, check_vma=False)
```

```python
import jax
import jax.numpy as jnp
from jax import lax
from jax.sharding import PartitionSpec as P
from jax.experimental import pallas as pl
from jax.experimental.pallas import tpu as pltpu

SWEEPS = 4
SUBIT = 2


tau_step = 0.22
fidelity = 0.1


def butterfly_sum(value, axes):
    for axis in axes:
        count = lax.axis_size(axis)
        if count & (count - 1):
            value = lax.psum(value, axis)
            continue
        step = 1
        while step < count:
            partner = lax.ppermute(value, axis, [(i, i ^ step) for i in range(count)])
            value = value + partner
            step *= 2
    return value


def with_halo(cells, axis, dim, width):
    count = lax.axis_size(axis)
    size = cells.shape[dim]
    head = lax.slice_in_dim(cells, 0, width, axis=dim)
    tail = lax.slice_in_dim(cells, size - width, size, axis=dim)
    before = lax.ppermute(tail, axis, [(i, i + 1) for i in range(count - 1)])
    after = lax.ppermute(head, axis, [(i + 1, i) for i in range(count - 1)])
    return jnp.concatenate([before, cells, after], axis=dim)


def inside_mask(axis, tile, width):
    count = lax.axis_size(axis)
    start = lax.axis_index(axis) * tile - width
    index = start + jnp.arange(tile + 2 * width, dtype=jnp.int32)
    return (index >= 0) & (index < count * tile)


def sweep(field, source, keep):
    diff_col = field[:-1, 1:] - field[:-1, :-1]
    diff_row = field[1:, :-1] - field[:-1, :-1]
    energy_sum = jnp.sum(diff_col * diff_col + diff_row * diff_row, axis=-1, keepdims=True)
    weight = 1.0 / jnp.sqrt(1.0 + energy_sum / field.shape[-1])
    flux_col = weight * diff_col
    flux_row = weight * diff_row
    spread = flux_col[1:, 1:] - flux_col[1:, :-1] + flux_row[1:, 1:] - flux_row[:-1, 1:]
    centre = field[1:-1, 1:-1]
    new = centre + tau_step * spread + tau_step * fidelity * (source - centre)
    return jnp.where(keep, new, 0.0)


def cholesky_qr(block):
    size = block.shape[1]
    inner = lax.dot_general(
        block, block, (((0,), (0,)), ((), ())),
        precision=lax.Precision.HIGHEST, preferred_element_type=jnp.float32,
    )
    sub = lax.broadcasted_iota(jnp.int32, (size, size), 0)
    lane = lax.broadcasted_iota(jnp.int32, (size, size), 1)
    lower = jnp.zeros((size, size), jnp.float32)
    upper = jnp.zeros((size, size), jnp.float32)
    rest = inner
    for j in range(size):
        col = jnp.sum(jnp.where(lane == j, rest, 0.0), axis=1, keepdims=True)
        row = jnp.sum(jnp.where(sub == j, rest, 0.0), axis=0, keepdims=True)
        pivot = jnp.sqrt(jnp.sum(jnp.where(lane[:1] == j, row, 0.0), axis=1, keepdims=True))
        col = jnp.where(sub[:, :1] >= j, col / pivot, 0.0)
        row = jnp.where(lane[:1] >= j, row / pivot, 0.0)
        lower = lower + jnp.where(lane == j, col, 0.0)
        upper = upper + jnp.where(sub == j, row, 0.0)
        rest = rest - col * row
    inverse = jnp.zeros((size, size), jnp.float32)
    for i in range(size):
        coef = jnp.sum(jnp.where(lane == i, upper, 0.0), axis=1, keepdims=True)
        diag = jnp.sum(jnp.where(sub[:, :1] == i, coef, 0.0), axis=0, keepdims=True)
        acc = jnp.sum(jnp.where(sub[:, :1] < i, coef, 0.0) * inverse, axis=0, keepdims=True)
        unit = jnp.where(lane[:1] == i, 1.0, 0.0)
        inverse = inverse + jnp.where(sub == i, (unit - acc) / diag, 0.0)
    return lax.dot_general(
        block, inverse, (((1,), (1,)), ((), ())),
        precision=lax.Precision.HIGHEST, preferred_element_type=jnp.float32,
    )


def subspace_kernel(gram_ref, basis_ref, out_ref):
    product = jnp.dot(
        gram_ref[...], basis_ref[...],
        precision=lax.Precision.HIGHEST, preferred_element_type=jnp.float32,
    )
    out_ref[...] = cholesky_qr(cholesky_qr(product))


def subspace_step(gram_full, basis):
    return pl.pallas_call(
        subspace_kernel,
        out_shape=jax.ShapeDtypeStruct(basis.shape, jnp.float32),
        cost_estimate=pl.CostEstimate(
            flops=2 * gram_full.shape[0] * gram_full.size + 8 * basis.size * basis.shape[1],
            transcendentals=2 * basis.shape[1],
            bytes_accessed=4 * (gram_full.size + 2 * basis.size),
        ),
    )(gram_full, basis)


def orthonormal(block):
    inner = jnp.dot(block.T, block, precision=lax.Precision.HIGHEST)
    lower = jnp.linalg.cholesky(inner)
    return lax.linalg.triangular_solve(lower, block, left_side=False, lower=True, transpose_a=True)


def shards(image, start_basis):
    band_count, tile_rows, tile_cols = image.shape
    width = SWEEPS
    cells = jnp.transpose(image, (1, 2, 0))
    ext = with_halo(cells, "row", 0, width)
    ext = with_halo(ext, "col", 1, width)
    row_in = inside_mask("row", tile_rows, width)
    col_in = inside_mask("col", tile_cols, width)
    field = ext
    for sweep_no in range(SWEEPS):
        left = width - sweep_no - 1
        lo = sweep_no + 1
        nr = tile_rows + 2 * left
        nc = tile_cols + 2 * left
        source = ext[lo:lo + nr, lo:lo + nc]
        keep = (row_in[lo:lo + nr, None] & col_in[None, lo:lo + nc])[:, :, None]
        field = sweep(field, source, keep)
    flat_cells = field.reshape(tile_rows * tile_cols, band_count)
    smoothed = jnp.transpose(field, (2, 0, 1))
    local_gram = lax.dot_general(
        flat_cells,
        flat_cells,
        (((0,), (0,)), ((), ())),
        precision=lax.Precision.HIGHEST,
        preferred_element_type=jnp.float32,
    )
    gram_full = butterfly_sum(local_gram, ("col", "row"))
    basis_now = start_basis
    for turn in range(SUBIT):
        basis_now = subspace_step(gram_full, basis_now)
    coeffs = jnp.dot(flat_cells, basis_now, precision=lax.Precision.HIGHEST)
    lowrank = lax.dot_general(
        basis_now,
        coeffs,
        (((1,), (1,)), ((), ())),
        precision=lax.Precision.HIGHEST,
    )
    return (smoothed, lowrank.reshape(band_count, tile_rows, tile_cols))


def solution(mesh):
    in_specs = (P(None, "row", "col"), P())
    out_specs = (P(None, "row", "col"), P(None, "row", "col"))
    return jax.shard_map(shards, mesh=mesh, in_specs=in_specs, out_specs=out_specs, check_vma=False)
```

```python
import functools

import jax
import jax.numpy as jnp
from jax import lax
from jax.sharding import PartitionSpec as P
from jax.experimental import pallas as pl
from jax.experimental.pallas import tpu as pltpu

SWEEPS = 4
SUBIT = 2


tau_step = 0.22
fidelity = 0.1


def butterfly_sum(value, axes, start=1):
    for axis in axes:
        count = lax.axis_size(axis)
        if count & (count - 1):
            value = lax.psum(value, axis)
            continue
        step = start if axis == axes[0] else 1
        while step < count:
            partner = lax.ppermute(value, axis, [(i, i ^ step) for i in range(count)])
            value = value + partner
            step *= 2
    return value


def paired_sum(value, axes):
    first = axes[0]
    count = lax.axis_size(first)
    half = value.shape[0] // 2
    if count < 2 or count & (count - 1) or value.shape[0] % 2:
        return butterfly_sum(value, axes)
    pairs = [(i, i ^ 1) for i in range(count)]
    low = lax.axis_index(first) % 2 == 0
    top, bottom = value[:half], value[half:]
    keep = jnp.where(low, top, bottom)
    give = jnp.where(low, bottom, top)
    part = keep + lax.ppermute(give, first, pairs)
    part = butterfly_sum(part, axes, start=2)
    other = lax.ppermute(part, first, pairs)
    return jnp.where(low, jnp.concatenate([part, other]), jnp.concatenate([other, part]))


def core_first(mesh):
    names = tuple(mesh.axis_names)
    devices = mesh.devices
    for pos, name in enumerate(names):
        if devices.shape[pos] < 2:
            continue
        at = [0] * devices.ndim
        one = devices[tuple(at)]
        at[pos] = 1
        two = devices[tuple(at)]
        coords = getattr(one, "coords", None)
        if coords is not None and tuple(coords) == tuple(getattr(two, "coords", ())):
            return (name,) + tuple(n for n in names if n != name)
    return names


def with_halo(cells, axis, dim, width):
    count = lax.axis_size(axis)
    size = cells.shape[dim]
    head = lax.slice_in_dim(cells, 0, width, axis=dim)
    tail = lax.slice_in_dim(cells, size - width, size, axis=dim)
    before = lax.ppermute(tail, axis, [(i, i + 1) for i in range(count - 1)])
    after = lax.ppermute(head, axis, [(i + 1, i) for i in range(count - 1)])
    return jnp.concatenate([before, cells, after], axis=dim)


def inside_mask(axis, tile, width):
    count = lax.axis_size(axis)
    start = lax.axis_index(axis) * tile - width
    index = start + jnp.arange(tile + 2 * width, dtype=jnp.int32)
    return (index >= 0) & (index < count * tile)


def sweep(field, source, keep):
    diff_col = field[:-1, 1:] - field[:-1, :-1]
    diff_row = field[1:, :-1] - field[:-1, :-1]
    energy_sum = jnp.sum(diff_col * diff_col + diff_row * diff_row, axis=-1, keepdims=True)
    weight = 1.0 / jnp.sqrt(1.0 + energy_sum / field.shape[-1])
    flux_col = weight * diff_col
    flux_row = weight * diff_row
    spread = flux_col[1:, 1:] - flux_col[1:, :-1] + flux_row[1:, 1:] - flux_row[:-1, 1:]
    centre = field[1:-1, 1:-1]
    new = centre + tau_step * spread + tau_step * fidelity * (source - centre)
    return jnp.where(keep, new, 0.0)


def cholesky_qr(block):
    size = block.shape[1]
    inner = lax.dot_general(
        block, block, (((0,), (0,)), ((), ())),
        precision=lax.Precision.HIGHEST, preferred_element_type=jnp.float32,
    )
    sub = lax.broadcasted_iota(jnp.int32, (size, size), 0)
    lane = lax.broadcasted_iota(jnp.int32, (size, size), 1)
    lower = jnp.zeros((size, size), jnp.float32)
    upper = jnp.zeros((size, size), jnp.float32)
    rest = inner
    for j in range(size):
        col = jnp.sum(jnp.where(lane == j, rest, 0.0), axis=1, keepdims=True)
        row = jnp.sum(jnp.where(sub == j, rest, 0.0), axis=0, keepdims=True)
        pivot = jnp.sqrt(jnp.sum(jnp.where(lane[:1] == j, row, 0.0), axis=1, keepdims=True))
        col = jnp.where(sub[:, :1] >= j, col / pivot, 0.0)
        row = jnp.where(lane[:1] >= j, row / pivot, 0.0)
        lower = lower + jnp.where(lane == j, col, 0.0)
        upper = upper + jnp.where(sub == j, row, 0.0)
        rest = rest - col * row
    inverse = jnp.zeros((size, size), jnp.float32)
    for i in range(size):
        coef = jnp.sum(jnp.where(lane == i, upper, 0.0), axis=1, keepdims=True)
        diag = jnp.sum(jnp.where(sub[:, :1] == i, coef, 0.0), axis=0, keepdims=True)
        acc = jnp.sum(jnp.where(sub[:, :1] < i, coef, 0.0) * inverse, axis=0, keepdims=True)
        unit = jnp.where(lane[:1] == i, 1.0, 0.0)
        inverse = inverse + jnp.where(sub == i, (unit - acc) / diag, 0.0)
    return lax.dot_general(
        block, inverse, (((1,), (1,)), ((), ())),
        precision=lax.Precision.HIGHEST, preferred_element_type=jnp.float32,
    )


def subspace_kernel(gram_ref, basis_ref, out_ref):
    product = jnp.dot(
        gram_ref[...], basis_ref[...],
        precision=lax.Precision.HIGHEST, preferred_element_type=jnp.float32,
    )
    out_ref[...] = cholesky_qr(cholesky_qr(product))


def subspace_step(gram_full, basis):
    return pl.pallas_call(
        subspace_kernel,
        out_shape=jax.ShapeDtypeStruct(basis.shape, jnp.float32),
        cost_estimate=pl.CostEstimate(
            flops=2 * gram_full.shape[0] * gram_full.size + 8 * basis.size * basis.shape[1],
            transcendentals=2 * basis.shape[1],
            bytes_accessed=4 * (gram_full.size + 2 * basis.size),
        ),
    )(gram_full, basis)


def orthonormal(block):
    inner = jnp.dot(block.T, block, precision=lax.Precision.HIGHEST)
    lower = jnp.linalg.cholesky(inner)
    return lax.linalg.triangular_solve(lower, block, left_side=False, lower=True, transpose_a=True)


def shards(order, image, start_basis):
    band_count, tile_rows, tile_cols = image.shape
    width = SWEEPS
    cells = jnp.transpose(image, (1, 2, 0))
    ext = with_halo(cells, "row", 0, width)
    ext = with_halo(ext, "col", 1, width)
    row_in = inside_mask("row", tile_rows, width)
    col_in = inside_mask("col", tile_cols, width)
    field = ext
    for sweep_no in range(SWEEPS):
        left = width - sweep_no - 1
        lo = sweep_no + 1
        nr = tile_rows + 2 * left
        nc = tile_cols + 2 * left
        source = ext[lo:lo + nr, lo:lo + nc]
        keep = (row_in[lo:lo + nr, None] & col_in[None, lo:lo + nc])[:, :, None]
        field = sweep(field, source, keep)
    flat_cells = field.reshape(tile_rows * tile_cols, band_count)
    smoothed = jnp.transpose(field, (2, 0, 1))
    local_gram = lax.dot_general(
        flat_cells,
        flat_cells,
        (((0,), (0,)), ((), ())),
        precision=lax.Precision.HIGHEST,
        preferred_element_type=jnp.float32,
    )
    gram_full = paired_sum(local_gram, order)
    basis_now = start_basis
    for turn in range(SUBIT):
        basis_now = subspace_step(gram_full, basis_now)
    coeffs = jnp.dot(flat_cells, basis_now, precision=lax.Precision.HIGHEST)
    lowrank = lax.dot_general(
        basis_now,
        coeffs,
        (((1,), (1,)), ((), ())),
        precision=lax.Precision.HIGHEST,
    )
    return (smoothed, lowrank.reshape(band_count, tile_rows, tile_cols))


def solution(mesh):
    in_specs = (P(None, "row", "col"), P())
    out_specs = (P(None, "row", "col"), P(None, "row", "col"))
    body = functools.partial(shards, core_first(mesh))
    return jax.shard_map(body, mesh=mesh, in_specs=in_specs, out_specs=out_specs, check_vma=False)
```

```python
import functools

import jax
import jax.numpy as jnp
from jax import lax
from jax.sharding import PartitionSpec as P
from jax.experimental import pallas as pl
from jax.experimental.pallas import tpu as pltpu

SWEEPS = 4
SUBIT = 2


tau_step = 0.22
fidelity = 0.1


def butterfly_sum(value, axes, start=1):
    for axis in axes:
        count = lax.axis_size(axis)
        if count & (count - 1):
            value = lax.psum(value, axis)
            continue
        step = start if axis == axes[0] else 1
        while step < count:
            partner = lax.ppermute(value, axis, [(i, i ^ step) for i in range(count)])
            value = value + partner
            step *= 2
    return value


def paired_sum(value, axes):
    first = axes[0]
    count = lax.axis_size(first)
    half = value.shape[0] // 2
    if count < 2 or count & (count - 1) or value.shape[0] % 2:
        return butterfly_sum(value, axes)
    pairs = [(i, i ^ 1) for i in range(count)]
    low = lax.axis_index(first) % 2 == 0
    top, bottom = value[:half], value[half:]
    keep = jnp.where(low, top, bottom)
    give = jnp.where(low, bottom, top)
    part = keep + lax.ppermute(give, first, pairs)
    part = butterfly_sum(part, axes, start=2)
    other = lax.ppermute(part, first, pairs)
    return jnp.where(low, jnp.concatenate([part, other]), jnp.concatenate([other, part]))


def core_first(mesh):
    names = tuple(mesh.axis_names)
    devices = mesh.devices
    for pos, name in enumerate(names):
        if devices.shape[pos] < 2:
            continue
        at = [0] * devices.ndim
        one = devices[tuple(at)]
        at[pos] = 1
        two = devices[tuple(at)]
        coords = getattr(one, "coords", None)
        if coords is not None and tuple(coords) == tuple(getattr(two, "coords", ())):
            return (name,) + tuple(n for n in names if n != name)
    return names


def with_halo(cells, axis, dim, width):
    count = lax.axis_size(axis)
    size = cells.shape[dim]
    head = lax.slice_in_dim(cells, 0, width, axis=dim)
    tail = lax.slice_in_dim(cells, size - width, size, axis=dim)
    before = lax.ppermute(tail, axis, [(i, i + 1) for i in range(count - 1)])
    after = lax.ppermute(head, axis, [(i + 1, i) for i in range(count - 1)])
    return jnp.concatenate([before, cells, after], axis=dim)


def with_ring(cells, width):
    rows_n = lax.axis_size("row")
    cols_n = lax.axis_size("col")
    tile_rows, tile_cols = cells.shape[0], cells.shape[1]

    def shift(block, down, across):
        pairs = [
            (r * cols_n + c, (r + down) * cols_n + c + across)
            for r in range(rows_n)
            for c in range(cols_n)
            if 0 <= r + down < rows_n and 0 <= c + across < cols_n
        ]
        return lax.ppermute(block, ("row", "col"), pairs)

    low_r, high_r = slice(0, width), slice(tile_rows - width, tile_rows)
    low_c, high_c = slice(0, width), slice(tile_cols - width, tile_cols)
    top = shift(cells[high_r], 1, 0)
    bottom = shift(cells[low_r], -1, 0)
    left = shift(cells[:, high_c], 0, 1)
    right = shift(cells[:, low_c], 0, -1)
    top_left = shift(cells[high_r, high_c], 1, 1)
    top_right = shift(cells[high_r, low_c], 1, -1)
    bottom_left = shift(cells[low_r, high_c], -1, 1)
    bottom_right = shift(cells[low_r, low_c], -1, -1)
    return jnp.concatenate(
        [
            jnp.concatenate([top_left, top, top_right], axis=1),
            jnp.concatenate([left, cells, right], axis=1),
            jnp.concatenate([bottom_left, bottom, bottom_right], axis=1),
        ],
        axis=0,
    )


def inside_mask(axis, tile, width):
    count = lax.axis_size(axis)
    start = lax.axis_index(axis) * tile - width
    index = start + jnp.arange(tile + 2 * width, dtype=jnp.int32)
    return (index >= 0) & (index < count * tile)


def sweep(field, source, keep):
    diff_col = field[:-1, 1:] - field[:-1, :-1]
    diff_row = field[1:, :-1] - field[:-1, :-1]
    energy_sum = jnp.sum(diff_col * diff_col + diff_row * diff_row, axis=-1, keepdims=True)
    weight = 1.0 / jnp.sqrt(1.0 + energy_sum / field.shape[-1])
    flux_col = weight * diff_col
    flux_row = weight * diff_row
    spread = flux_col[1:, 1:] - flux_col[1:, :-1] + flux_row[1:, 1:] - flux_row[:-1, 1:]
    centre = field[1:-1, 1:-1]
    new = centre + tau_step * spread + tau_step * fidelity * (source - centre)
    return jnp.where(keep, new, 0.0)


def cholesky_qr(block):
    size = block.shape[1]
    inner = lax.dot_general(
        block, block, (((0,), (0,)), ((), ())),
        precision=lax.Precision.HIGHEST, preferred_element_type=jnp.float32,
    )
    sub = lax.broadcasted_iota(jnp.int32, (size, size), 0)
    lane = lax.broadcasted_iota(jnp.int32, (size, size), 1)
    lower = jnp.zeros((size, size), jnp.float32)
    upper = jnp.zeros((size, size), jnp.float32)
    rest = inner
    for j in range(size):
        col = jnp.sum(jnp.where(lane == j, rest, 0.0), axis=1, keepdims=True)
        row = jnp.sum(jnp.where(sub == j, rest, 0.0), axis=0, keepdims=True)
        pivot = jnp.sqrt(jnp.sum(jnp.where(lane[:1] == j, row, 0.0), axis=1, keepdims=True))
        col = jnp.where(sub[:, :1] >= j, col / pivot, 0.0)
        row = jnp.where(lane[:1] >= j, row / pivot, 0.0)
        lower = lower + jnp.where(lane == j, col, 0.0)
        upper = upper + jnp.where(sub == j, row, 0.0)
        rest = rest - col * row
    inverse = jnp.zeros((size, size), jnp.float32)
    for i in range(size):
        coef = jnp.sum(jnp.where(lane == i, upper, 0.0), axis=1, keepdims=True)
        diag = jnp.sum(jnp.where(sub[:, :1] == i, coef, 0.0), axis=0, keepdims=True)
        acc = jnp.sum(jnp.where(sub[:, :1] < i, coef, 0.0) * inverse, axis=0, keepdims=True)
        unit = jnp.where(lane[:1] == i, 1.0, 0.0)
        inverse = inverse + jnp.where(sub == i, (unit - acc) / diag, 0.0)
    return lax.dot_general(
        block, inverse, (((1,), (1,)), ((), ())),
        precision=lax.Precision.HIGHEST, preferred_element_type=jnp.float32,
    )


def subspace_kernel(gram_ref, basis_ref, out_ref):
    product = jnp.dot(
        gram_ref[...], basis_ref[...],
        precision=lax.Precision.HIGHEST, preferred_element_type=jnp.float32,
    )
    out_ref[...] = cholesky_qr(cholesky_qr(product))


def subspace_step(gram_full, basis):
    return pl.pallas_call(
        subspace_kernel,
        out_shape=jax.ShapeDtypeStruct(basis.shape, jnp.float32),
        cost_estimate=pl.CostEstimate(
            flops=2 * gram_full.shape[0] * gram_full.size + 8 * basis.size * basis.shape[1],
            transcendentals=2 * basis.shape[1],
            bytes_accessed=4 * (gram_full.size + 2 * basis.size),
        ),
    )(gram_full, basis)


def orthonormal(block):
    inner = jnp.dot(block.T, block, precision=lax.Precision.HIGHEST)
    lower = jnp.linalg.cholesky(inner)
    return lax.linalg.triangular_solve(lower, block, left_side=False, lower=True, transpose_a=True)


def shards(order, image, start_basis):
    band_count, tile_rows, tile_cols = image.shape
    width = SWEEPS
    cells = jnp.transpose(image, (1, 2, 0))
    ext = with_ring(cells, width)
    row_in = inside_mask("row", tile_rows, width)
    col_in = inside_mask("col", tile_cols, width)
    field = ext
    for sweep_no in range(SWEEPS):
        left = width - sweep_no - 1
        lo = sweep_no + 1
        nr = tile_rows + 2 * left
        nc = tile_cols + 2 * left
        source = ext[lo:lo + nr, lo:lo + nc]
        keep = (row_in[lo:lo + nr, None] & col_in[None, lo:lo + nc])[:, :, None]
        field = sweep(field, source, keep)
    flat_cells = field.reshape(tile_rows * tile_cols, band_count)
    smoothed = jnp.transpose(field, (2, 0, 1))
    local_gram = lax.dot_general(
        flat_cells,
        flat_cells,
        (((0,), (0,)), ((), ())),
        precision=lax.Precision.HIGHEST,
        preferred_element_type=jnp.float32,
    )
    gram_full = paired_sum(local_gram, order)
    basis_now = start_basis
    for turn in range(SUBIT):
        basis_now = subspace_step(gram_full, basis_now)
    coeffs = jnp.dot(flat_cells, basis_now, precision=lax.Precision.HIGHEST)
    lowrank = lax.dot_general(
        basis_now,
        coeffs,
        (((1,), (1,)), ((), ())),
        precision=lax.Precision.HIGHEST,
    )
    return (smoothed, lowrank.reshape(band_count, tile_rows, tile_cols))


def solution(mesh):
    in_specs = (P(None, "row", "col"), P())
    out_specs = (P(None, "row", "col"), P(None, "row", "col"))
    body = functools.partial(shards, core_first(mesh))
    return jax.shard_map(body, mesh=mesh, in_specs=in_specs, out_specs=out_specs, check_vma=False)
```

```python
import functools

import jax
import jax.numpy as jnp
from jax import lax
from jax.sharding import PartitionSpec as P
from jax.experimental import pallas as pl
from jax.experimental.pallas import tpu as pltpu

SWEEPS = 4
SUBIT = 2


tau_step = 0.22
fidelity = 0.1


def butterfly_sum(value, axes, start=1):
    for axis in axes:
        count = lax.axis_size(axis)
        if count & (count - 1):
            value = lax.psum(value, axis)
            continue
        step = start if axis == axes[0] else 1
        while step < count:
            partner = lax.ppermute(value, axis, [(i, i ^ step) for i in range(count)])
            value = value + partner
            step *= 2
    return value


def paired_sum(value, axes):
    first = axes[0]
    count = lax.axis_size(first)
    half = value.shape[0] // 2
    if count < 2 or count & (count - 1) or value.shape[0] % 2:
        return butterfly_sum(value, axes)
    pairs = [(i, i ^ 1) for i in range(count)]
    low = lax.axis_index(first) % 2 == 0
    top, bottom = value[:half], value[half:]
    keep = jnp.where(low, top, bottom)
    give = jnp.where(low, bottom, top)
    part = keep + lax.ppermute(give, first, pairs)
    part = butterfly_sum(part, axes, start=2)
    other = lax.ppermute(part, first, pairs)
    return jnp.where(low, jnp.concatenate([part, other]), jnp.concatenate([other, part]))


def core_first(mesh):
    names = tuple(mesh.axis_names)
    devices = mesh.devices
    for pos, name in enumerate(names):
        if devices.shape[pos] < 2:
            continue
        at = [0] * devices.ndim
        one = devices[tuple(at)]
        at[pos] = 1
        two = devices[tuple(at)]
        coords = getattr(one, "coords", None)
        if coords is not None and tuple(coords) == tuple(getattr(two, "coords", ())):
            return (name,) + tuple(n for n in names if n != name)
    return names


def with_halo(cells, axis, dim, width):
    count = lax.axis_size(axis)
    size = cells.shape[dim]
    head = lax.slice_in_dim(cells, 0, width, axis=dim)
    tail = lax.slice_in_dim(cells, size - width, size, axis=dim)
    before = lax.ppermute(tail, axis, [(i, i + 1) for i in range(count - 1)])
    after = lax.ppermute(head, axis, [(i + 1, i) for i in range(count - 1)])
    return jnp.concatenate([before, cells, after], axis=dim)


def with_ring(cells, width):
    rows_n = lax.axis_size("row")
    cols_n = lax.axis_size("col")
    tile_rows, tile_cols = cells.shape[0], cells.shape[1]
    down = [(i, i + 1) for i in range(rows_n - 1)]
    up = [(i + 1, i) for i in range(rows_n - 1)]
    right = [(i, i + 1) for i in range(cols_n - 1)]
    left = [(i + 1, i) for i in range(cols_n - 1)]
    top = lax.ppermute(cells[tile_rows - width:], "row", down)
    bottom = lax.ppermute(cells[:width], "row", up)
    west = lax.ppermute(cells[:, tile_cols - width:], "col", right)
    east = lax.ppermute(cells[:, :width], "col", left)
    rims = jnp.concatenate([top, bottom], axis=0)
    rim_west = lax.ppermute(rims[:, tile_cols - width:], "col", right)
    rim_east = lax.ppermute(rims[:, :width], "col", left)
    return jnp.concatenate(
        [
            jnp.concatenate([rim_west[:width], top, rim_east[:width]], axis=1),
            jnp.concatenate([west, cells, east], axis=1),
            jnp.concatenate([rim_west[width:], bottom, rim_east[width:]], axis=1),
        ],
        axis=0,
    )


def inside_mask(axis, tile, width):
    count = lax.axis_size(axis)
    start = lax.axis_index(axis) * tile - width
    index = start + jnp.arange(tile + 2 * width, dtype=jnp.int32)
    return (index >= 0) & (index < count * tile)


def sweep(field, source, keep):
    diff_col = field[:-1, 1:] - field[:-1, :-1]
    diff_row = field[1:, :-1] - field[:-1, :-1]
    energy_sum = jnp.sum(diff_col * diff_col + diff_row * diff_row, axis=-1, keepdims=True)
    weight = 1.0 / jnp.sqrt(1.0 + energy_sum / field.shape[-1])
    flux_col = weight * diff_col
    flux_row = weight * diff_row
    spread = flux_col[1:, 1:] - flux_col[1:, :-1] + flux_row[1:, 1:] - flux_row[:-1, 1:]
    centre = field[1:-1, 1:-1]
    new = centre + tau_step * spread + tau_step * fidelity * (source - centre)
    return jnp.where(keep, new, 0.0)


def cholesky_qr(block):
    size = block.shape[1]
    inner = lax.dot_general(
        block, block, (((0,), (0,)), ((), ())),
        precision=lax.Precision.HIGHEST, preferred_element_type=jnp.float32,
    )
    sub = lax.broadcasted_iota(jnp.int32, (size, size), 0)
    lane = lax.broadcasted_iota(jnp.int32, (size, size), 1)
    lower = jnp.zeros((size, size), jnp.float32)
    upper = jnp.zeros((size, size), jnp.float32)
    rest = inner
    for j in range(size):
        col = jnp.sum(jnp.where(lane == j, rest, 0.0), axis=1, keepdims=True)
        row = jnp.sum(jnp.where(sub == j, rest, 0.0), axis=0, keepdims=True)
        pivot = jnp.sqrt(jnp.sum(jnp.where(lane[:1] == j, row, 0.0), axis=1, keepdims=True))
        col = jnp.where(sub[:, :1] >= j, col / pivot, 0.0)
        row = jnp.where(lane[:1] >= j, row / pivot, 0.0)
        lower = lower + jnp.where(lane == j, col, 0.0)
        upper = upper + jnp.where(sub == j, row, 0.0)
        rest = rest - col * row
    inverse = jnp.zeros((size, size), jnp.float32)
    for i in range(size):
        coef = jnp.sum(jnp.where(lane == i, upper, 0.0), axis=1, keepdims=True)
        diag = jnp.sum(jnp.where(sub[:, :1] == i, coef, 0.0), axis=0, keepdims=True)
        acc = jnp.sum(jnp.where(sub[:, :1] < i, coef, 0.0) * inverse, axis=0, keepdims=True)
        unit = jnp.where(lane[:1] == i, 1.0, 0.0)
        inverse = inverse + jnp.where(sub == i, (unit - acc) / diag, 0.0)
    return lax.dot_general(
        block, inverse, (((1,), (1,)), ((), ())),
        precision=lax.Precision.HIGHEST, preferred_element_type=jnp.float32,
    )


def subspace_kernel(gram_ref, basis_ref, out_ref):
    product = jnp.dot(
        gram_ref[...], basis_ref[...],
        precision=lax.Precision.HIGHEST, preferred_element_type=jnp.float32,
    )
    out_ref[...] = cholesky_qr(cholesky_qr(product))


def subspace_step(gram_full, basis):
    return pl.pallas_call(
        subspace_kernel,
        out_shape=jax.ShapeDtypeStruct(basis.shape, jnp.float32),
        cost_estimate=pl.CostEstimate(
            flops=2 * gram_full.shape[0] * gram_full.size + 8 * basis.size * basis.shape[1],
            transcendentals=2 * basis.shape[1],
            bytes_accessed=4 * (gram_full.size + 2 * basis.size),
        ),
    )(gram_full, basis)


def orthonormal(block):
    inner = jnp.dot(block.T, block, precision=lax.Precision.HIGHEST)
    lower = jnp.linalg.cholesky(inner)
    return lax.linalg.triangular_solve(lower, block, left_side=False, lower=True, transpose_a=True)


def shards(order, image, start_basis):
    band_count, tile_rows, tile_cols = image.shape
    width = SWEEPS
    cells = jnp.transpose(image, (1, 2, 0))
    ext = with_ring(cells, width)
    row_in = inside_mask("row", tile_rows, width)
    col_in = inside_mask("col", tile_cols, width)
    field = ext
    for sweep_no in range(SWEEPS):
        left = width - sweep_no - 1
        lo = sweep_no + 1
        nr = tile_rows + 2 * left
        nc = tile_cols + 2 * left
        source = ext[lo:lo + nr, lo:lo + nc]
        keep = (row_in[lo:lo + nr, None] & col_in[None, lo:lo + nc])[:, :, None]
        field = sweep(field, source, keep)
    flat_cells = field.reshape(tile_rows * tile_cols, band_count)
    smoothed = jnp.transpose(field, (2, 0, 1))
    local_gram = lax.dot_general(
        flat_cells,
        flat_cells,
        (((0,), (0,)), ((), ())),
        precision=lax.Precision.HIGHEST,
        preferred_element_type=jnp.float32,
    )
    gram_full = paired_sum(local_gram, order)
    basis_now = start_basis
    for turn in range(SUBIT):
        basis_now = subspace_step(gram_full, basis_now)
    coeffs = jnp.dot(flat_cells, basis_now, precision=lax.Precision.HIGHEST)
    lowrank = lax.dot_general(
        basis_now,
        coeffs,
        (((1,), (1,)), ((), ())),
        precision=lax.Precision.HIGHEST,
    )
    return (smoothed, lowrank.reshape(band_count, tile_rows, tile_cols))


def solution(mesh):
    in_specs = (P(None, "row", "col"), P())
    out_specs = (P(None, "row", "col"), P(None, "row", "col"))
    body = functools.partial(shards, core_first(mesh))
    return jax.shard_map(body, mesh=mesh, in_specs=in_specs, out_specs=out_specs, check_vma=False)
```

```python
import functools

import jax
import jax.numpy as jnp
from jax import lax
from jax.sharding import PartitionSpec as P
from jax.experimental import pallas as pl
from jax.experimental.layout import Layout, with_layout_constraint
from jax.experimental.pallas import tpu as pltpu

SWEEPS = 4
SUBIT = 2


tau_step = 0.22
fidelity = 0.1


def butterfly_sum(value, axes, start=1):
    for axis in axes:
        count = lax.axis_size(axis)
        if count & (count - 1):
            value = lax.psum(value, axis)
            continue
        step = start if axis == axes[0] else 1
        while step < count:
            partner = lax.ppermute(value, axis, [(i, i ^ step) for i in range(count)])
            value = value + partner
            step *= 2
    return value


def paired_sum(value, axes):
    first = axes[0]
    count = lax.axis_size(first)
    half = value.shape[0] // 2
    if count < 2 or count & (count - 1) or value.shape[0] % 2:
        return butterfly_sum(value, axes)
    pairs = [(i, i ^ 1) for i in range(count)]
    low = lax.axis_index(first) % 2 == 0
    top, bottom = value[:half], value[half:]
    keep = jnp.where(low, top, bottom)
    give = jnp.where(low, bottom, top)
    part = keep + lax.ppermute(give, first, pairs)
    part = butterfly_sum(part, axes, start=2)
    other = lax.ppermute(part, first, pairs)
    return jnp.where(low, jnp.concatenate([part, other]), jnp.concatenate([other, part]))


def core_first(mesh):
    names = tuple(mesh.axis_names)
    devices = mesh.devices
    for pos, name in enumerate(names):
        if devices.shape[pos] < 2:
            continue
        at = [0] * devices.ndim
        one = devices[tuple(at)]
        at[pos] = 1
        two = devices[tuple(at)]
        coords = getattr(one, "coords", None)
        if coords is not None and tuple(coords) == tuple(getattr(two, "coords", ())):
            return (name,) + tuple(n for n in names if n != name)
    return names


def with_halo(cells, axis, dim, width):
    count = lax.axis_size(axis)
    size = cells.shape[dim]
    head = lax.slice_in_dim(cells, 0, width, axis=dim)
    tail = lax.slice_in_dim(cells, size - width, size, axis=dim)
    before = lax.ppermute(tail, axis, [(i, i + 1) for i in range(count - 1)])
    after = lax.ppermute(head, axis, [(i + 1, i) for i in range(count - 1)])
    return jnp.concatenate([before, cells, after], axis=dim)


def pinned(cells):
    return with_layout_constraint(cells, Layout(major_to_minor=tuple(range(cells.ndim))))


def inside_mask(axis, tile, width):
    count = lax.axis_size(axis)
    start = lax.axis_index(axis) * tile - width
    index = start + jnp.arange(tile + 2 * width, dtype=jnp.int32)
    return (index >= 0) & (index < count * tile)


def sweep(field, source, keep):
    diff_col = field[:-1, 1:] - field[:-1, :-1]
    diff_row = field[1:, :-1] - field[:-1, :-1]
    energy_sum = jnp.sum(diff_col * diff_col + diff_row * diff_row, axis=-1, keepdims=True)
    weight = 1.0 / jnp.sqrt(1.0 + energy_sum / field.shape[-1])
    flux_col = weight * diff_col
    flux_row = weight * diff_row
    spread = flux_col[1:, 1:] - flux_col[1:, :-1] + flux_row[1:, 1:] - flux_row[:-1, 1:]
    centre = field[1:-1, 1:-1]
    new = centre + tau_step * spread + tau_step * fidelity * (source - centre)
    return jnp.where(keep, new, 0.0)


def cholesky_qr(block):
    size = block.shape[1]
    inner = lax.dot_general(
        block, block, (((0,), (0,)), ((), ())),
        precision=lax.Precision.HIGHEST, preferred_element_type=jnp.float32,
    )
    sub = lax.broadcasted_iota(jnp.int32, (size, size), 0)
    lane = lax.broadcasted_iota(jnp.int32, (size, size), 1)
    lower = jnp.zeros((size, size), jnp.float32)
    upper = jnp.zeros((size, size), jnp.float32)
    rest = inner
    for j in range(size):
        col = jnp.sum(jnp.where(lane == j, rest, 0.0), axis=1, keepdims=True)
        row = jnp.sum(jnp.where(sub == j, rest, 0.0), axis=0, keepdims=True)
        pivot = jnp.sqrt(jnp.sum(jnp.where(lane[:1] == j, row, 0.0), axis=1, keepdims=True))
        col = jnp.where(sub[:, :1] >= j, col / pivot, 0.0)
        row = jnp.where(lane[:1] >= j, row / pivot, 0.0)
        lower = lower + jnp.where(lane == j, col, 0.0)
        upper = upper + jnp.where(sub == j, row, 0.0)
        rest = rest - col * row
    inverse = jnp.zeros((size, size), jnp.float32)
    for i in range(size):
        coef = jnp.sum(jnp.where(lane == i, upper, 0.0), axis=1, keepdims=True)
        diag = jnp.sum(jnp.where(sub[:, :1] == i, coef, 0.0), axis=0, keepdims=True)
        acc = jnp.sum(jnp.where(sub[:, :1] < i, coef, 0.0) * inverse, axis=0, keepdims=True)
        unit = jnp.where(lane[:1] == i, 1.0, 0.0)
        inverse = inverse + jnp.where(sub == i, (unit - acc) / diag, 0.0)
    return lax.dot_general(
        block, inverse, (((1,), (1,)), ((), ())),
        precision=lax.Precision.HIGHEST, preferred_element_type=jnp.float32,
    )


def subspace_kernel(gram_ref, basis_ref, out_ref):
    product = jnp.dot(
        gram_ref[...], basis_ref[...],
        precision=lax.Precision.HIGHEST, preferred_element_type=jnp.float32,
    )
    out_ref[...] = cholesky_qr(cholesky_qr(product))


def subspace_step(gram_full, basis):
    return pl.pallas_call(
        subspace_kernel,
        out_shape=jax.ShapeDtypeStruct(basis.shape, jnp.float32),
        cost_estimate=pl.CostEstimate(
            flops=2 * gram_full.shape[0] * gram_full.size + 8 * basis.size * basis.shape[1],
            transcendentals=2 * basis.shape[1],
            bytes_accessed=4 * (gram_full.size + 2 * basis.size),
        ),
    )(gram_full, basis)


def orthonormal(block):
    inner = jnp.dot(block.T, block, precision=lax.Precision.HIGHEST)
    lower = jnp.linalg.cholesky(inner)
    return lax.linalg.triangular_solve(lower, block, left_side=False, lower=True, transpose_a=True)


def shards(order, image, start_basis):
    band_count, tile_rows, tile_cols = image.shape
    width = SWEEPS
    cells = pinned(jnp.transpose(image, (1, 2, 0)))
    ext = with_halo(cells, "row", 0, width)
    ext = with_halo(ext, "col", 1, width)
    row_in = inside_mask("row", tile_rows, width)
    col_in = inside_mask("col", tile_cols, width)
    field = ext
    for sweep_no in range(SWEEPS):
        left = width - sweep_no - 1
        lo = sweep_no + 1
        nr = tile_rows + 2 * left
        nc = tile_cols + 2 * left
        source = ext[lo:lo + nr, lo:lo + nc]
        keep = (row_in[lo:lo + nr, None] & col_in[None, lo:lo + nc])[:, :, None]
        field = pinned(sweep(field, source, keep))
    flat_cells = field.reshape(tile_rows * tile_cols, band_count)
    smoothed = jnp.transpose(field, (2, 0, 1))
    local_gram = lax.dot_general(
        flat_cells,
        flat_cells,
        (((0,), (0,)), ((), ())),
        precision=lax.Precision.HIGHEST,
        preferred_element_type=jnp.float32,
    )
    gram_full = paired_sum(local_gram, order)
    basis_now = start_basis
    for turn in range(SUBIT):
        basis_now = subspace_step(gram_full, basis_now)
    coeffs = jnp.dot(flat_cells, basis_now, precision=lax.Precision.HIGHEST)
    lowrank = lax.dot_general(
        basis_now,
        coeffs,
        (((1,), (1,)), ((), ())),
        precision=lax.Precision.HIGHEST,
    )
    return (smoothed, lowrank.reshape(band_count, tile_rows, tile_cols))


def solution(mesh):
    in_specs = (P(None, "row", "col"), P())
    out_specs = (P(None, "row", "col"), P(None, "row", "col"))
    body = functools.partial(shards, core_first(mesh))
    return jax.shard_map(body, mesh=mesh, in_specs=in_specs, out_specs=out_specs, check_vma=False)
```

```python
import functools

import jax
import jax.numpy as jnp
from jax import lax
from jax.sharding import PartitionSpec as P
from jax.experimental import pallas as pl
from jax.experimental.layout import Layout, with_layout_constraint
from jax.experimental.pallas import tpu as pltpu

SWEEPS = 4
SUBIT = 2


tau_step = 0.22
fidelity = 0.1


def butterfly_sum(value, axes, start=1):
    for axis in axes:
        count = lax.axis_size(axis)
        if count & (count - 1):
            value = lax.psum(value, axis)
            continue
        step = start if axis == axes[0] else 1
        while step < count:
            partner = lax.ppermute(value, axis, [(i, i ^ step) for i in range(count)])
            value = value + partner
            step *= 2
    return value


def paired_sum(value, axes):
    first = axes[0]
    count = lax.axis_size(first)
    half = value.shape[0] // 2
    if count < 2 or count & (count - 1) or value.shape[0] % 2:
        return butterfly_sum(value, axes)
    pairs = [(i, i ^ 1) for i in range(count)]
    low = lax.axis_index(first) % 2 == 0
    top, bottom = value[:half], value[half:]
    keep = jnp.where(low, top, bottom)
    give = jnp.where(low, bottom, top)
    part = keep + lax.ppermute(give, first, pairs)
    part = butterfly_sum(part, axes, start=2)
    other = lax.ppermute(part, first, pairs)
    return jnp.where(low, jnp.concatenate([part, other]), jnp.concatenate([other, part]))


def core_first(mesh):
    names = tuple(mesh.axis_names)
    devices = mesh.devices
    for pos, name in enumerate(names):
        if devices.shape[pos] < 2:
            continue
        at = [0] * devices.ndim
        one = devices[tuple(at)]
        at[pos] = 1
        two = devices[tuple(at)]
        coords = getattr(one, "coords", None)
        if coords is not None and tuple(coords) == tuple(getattr(two, "coords", ())):
            return (name,) + tuple(n for n in names if n != name)
    return names


def flat_permute(block, axis, pairs):
    pixels = block.size // block.shape[-1]
    if pixels % 64 or pixels <= block.shape[-1]:
        return lax.ppermute(block, axis, pairs)
    flat = block.reshape(pixels // 64, 64, block.shape[-1])
    return lax.ppermute(flat, axis, pairs).reshape(block.shape)


def with_halo(cells, axis, dim, width):
    count = lax.axis_size(axis)
    size = cells.shape[dim]
    head = lax.slice_in_dim(cells, 0, width, axis=dim)
    tail = lax.slice_in_dim(cells, size - width, size, axis=dim)
    before = flat_permute(tail, axis, [(i, i + 1) for i in range(count - 1)])
    after = flat_permute(head, axis, [(i + 1, i) for i in range(count - 1)])
    return jnp.concatenate([before, cells, after], axis=dim)


def pinned(cells):
    return with_layout_constraint(cells, Layout(major_to_minor=tuple(range(cells.ndim))))


def inside_mask(axis, tile, width):
    count = lax.axis_size(axis)
    start = lax.axis_index(axis) * tile - width
    index = start + jnp.arange(tile + 2 * width, dtype=jnp.int32)
    return (index >= 0) & (index < count * tile)


def sweep(field, source, keep):
    diff_col = field[:-1, 1:] - field[:-1, :-1]
    diff_row = field[1:, :-1] - field[:-1, :-1]
    energy_sum = jnp.sum(diff_col * diff_col + diff_row * diff_row, axis=-1, keepdims=True)
    weight = 1.0 / jnp.sqrt(1.0 + energy_sum / field.shape[-1])
    flux_col = weight * diff_col
    flux_row = weight * diff_row
    spread = flux_col[1:, 1:] - flux_col[1:, :-1] + flux_row[1:, 1:] - flux_row[:-1, 1:]
    centre = field[1:-1, 1:-1]
    new = centre + tau_step * spread + tau_step * fidelity * (source - centre)
    return jnp.where(keep, new, 0.0)


def cholesky_qr(block):
    size = block.shape[1]
    inner = lax.dot_general(
        block, block, (((0,), (0,)), ((), ())),
        precision=lax.Precision.HIGHEST, preferred_element_type=jnp.float32,
    )
    sub = lax.broadcasted_iota(jnp.int32, (size, size), 0)
    lane = lax.broadcasted_iota(jnp.int32, (size, size), 1)
    lower = jnp.zeros((size, size), jnp.float32)
    upper = jnp.zeros((size, size), jnp.float32)
    rest = inner
    for j in range(size):
        col = jnp.sum(jnp.where(lane == j, rest, 0.0), axis=1, keepdims=True)
        row = jnp.sum(jnp.where(sub == j, rest, 0.0), axis=0, keepdims=True)
        pivot = jnp.sqrt(jnp.sum(jnp.where(lane[:1] == j, row, 0.0), axis=1, keepdims=True))
        col = jnp.where(sub[:, :1] >= j, col / pivot, 0.0)
        row = jnp.where(lane[:1] >= j, row / pivot, 0.0)
        lower = lower + jnp.where(lane == j, col, 0.0)
        upper = upper + jnp.where(sub == j, row, 0.0)
        rest = rest - col * row
    inverse = jnp.zeros((size, size), jnp.float32)
    for i in range(size):
        coef = jnp.sum(jnp.where(lane == i, upper, 0.0), axis=1, keepdims=True)
        diag = jnp.sum(jnp.where(sub[:, :1] == i, coef, 0.0), axis=0, keepdims=True)
        acc = jnp.sum(jnp.where(sub[:, :1] < i, coef, 0.0) * inverse, axis=0, keepdims=True)
        unit = jnp.where(lane[:1] == i, 1.0, 0.0)
        inverse = inverse + jnp.where(sub == i, (unit - acc) / diag, 0.0)
    return lax.dot_general(
        block, inverse, (((1,), (1,)), ((), ())),
        precision=lax.Precision.HIGHEST, preferred_element_type=jnp.float32,
    )


def subspace_kernel(gram_ref, basis_ref, out_ref):
    product = jnp.dot(
        gram_ref[...], basis_ref[...],
        precision=lax.Precision.HIGHEST, preferred_element_type=jnp.float32,
    )
    out_ref[...] = cholesky_qr(cholesky_qr(product))


def subspace_step(gram_full, basis):
    return pl.pallas_call(
        subspace_kernel,
        out_shape=jax.ShapeDtypeStruct(basis.shape, jnp.float32),
        cost_estimate=pl.CostEstimate(
            flops=2 * gram_full.shape[0] * gram_full.size + 8 * basis.size * basis.shape[1],
            transcendentals=2 * basis.shape[1],
            bytes_accessed=4 * (gram_full.size + 2 * basis.size),
        ),
    )(gram_full, basis)


def orthonormal(block):
    inner = jnp.dot(block.T, block, precision=lax.Precision.HIGHEST)
    lower = jnp.linalg.cholesky(inner)
    return lax.linalg.triangular_solve(lower, block, left_side=False, lower=True, transpose_a=True)


def shards(order, image, start_basis):
    band_count, tile_rows, tile_cols = image.shape
    width = SWEEPS
    cells = pinned(jnp.transpose(image, (1, 2, 0)))
    ext = with_halo(cells, "row", 0, width)
    ext = with_halo(ext, "col", 1, width)
    row_in = inside_mask("row", tile_rows, width)
    col_in = inside_mask("col", tile_cols, width)
    field = ext
    for sweep_no in range(SWEEPS):
        left = width - sweep_no - 1
        lo = sweep_no + 1
        nr = tile_rows + 2 * left
        nc = tile_cols + 2 * left
        source = ext[lo:lo + nr, lo:lo + nc]
        keep = (row_in[lo:lo + nr, None] & col_in[None, lo:lo + nc])[:, :, None]
        field = pinned(sweep(field, source, keep))
    flat_cells = field.reshape(tile_rows * tile_cols, band_count)
    smoothed = jnp.transpose(field, (2, 0, 1))
    local_gram = lax.dot_general(
        flat_cells,
        flat_cells,
        (((0,), (0,)), ((), ())),
        precision=lax.Precision.HIGHEST,
        preferred_element_type=jnp.float32,
    )
    gram_full = paired_sum(local_gram, order)
    basis_now = start_basis
    for turn in range(SUBIT):
        basis_now = subspace_step(gram_full, basis_now)
    coeffs = jnp.dot(flat_cells, basis_now, precision=lax.Precision.HIGHEST)
    lowrank = lax.dot_general(
        basis_now,
        coeffs,
        (((1,), (1,)), ((), ())),
        precision=lax.Precision.HIGHEST,
    )
    return (smoothed, lowrank.reshape(band_count, tile_rows, tile_cols))


def solution(mesh):
    in_specs = (P(None, "row", "col"), P())
    out_specs = (P(None, "row", "col"), P(None, "row", "col"))
    body = functools.partial(shards, core_first(mesh))
    return jax.shard_map(body, mesh=mesh, in_specs=in_specs, out_specs=out_specs, check_vma=False)
```

```python
import functools

import jax
import jax.numpy as jnp
from jax import lax
from jax.sharding import PartitionSpec as P
from jax.experimental import pallas as pl
from jax.experimental.layout import Layout, with_layout_constraint
from jax.experimental.pallas import tpu as pltpu

SWEEPS = 4
SUBIT = 2


tau_step = 0.22
fidelity = 0.1


def butterfly_sum(value, axes, start=1):
    for axis in axes:
        count = lax.axis_size(axis)
        if count & (count - 1):
            value = lax.psum(value, axis)
            continue
        step = start if axis == axes[0] else 1
        while step < count:
            partner = lax.ppermute(value, axis, [(i, i ^ step) for i in range(count)])
            value = value + partner
            step *= 2
    return value


def paired_sum(value, axes):
    first = axes[0]
    count = lax.axis_size(first)
    half = value.shape[0] // 2
    if count < 2 or count & (count - 1) or value.shape[0] % 2:
        return butterfly_sum(value, axes)
    pairs = [(i, i ^ 1) for i in range(count)]
    low = lax.axis_index(first) % 2 == 0
    top, bottom = value[:half], value[half:]
    keep = jnp.where(low, top, bottom)
    give = jnp.where(low, bottom, top)
    part = keep + lax.ppermute(give, first, pairs)
    part = butterfly_sum(part, axes, start=2)
    other = lax.ppermute(part, first, pairs)
    return jnp.where(low, jnp.concatenate([part, other]), jnp.concatenate([other, part]))


def core_first(mesh):
    names = tuple(mesh.axis_names)
    devices = mesh.devices
    for pos, name in enumerate(names):
        if devices.shape[pos] < 2:
            continue
        at = [0] * devices.ndim
        one = devices[tuple(at)]
        at[pos] = 1
        two = devices[tuple(at)]
        coords = getattr(one, "coords", None)
        if coords is not None and tuple(coords) == tuple(getattr(two, "coords", ())):
            return (name,) + tuple(n for n in names if n != name)
    return names


def flat_permute(block, axis, pairs):
    pixels = block.size // block.shape[-1]
    if pixels % 64 or pixels <= block.shape[-1]:
        return lax.ppermute(block, axis, pairs)
    flat = block.reshape(pixels // 64, 64, block.shape[-1])
    return lax.ppermute(flat, axis, pairs).reshape(block.shape)


def with_halo(cells, axis, dim, width):
    count = lax.axis_size(axis)
    size = cells.shape[dim]
    head = lax.slice_in_dim(cells, 0, width, axis=dim)
    tail = lax.slice_in_dim(cells, size - width, size, axis=dim)
    before = flat_permute(tail, axis, [(i, i + 1) for i in range(count - 1)])
    after = flat_permute(head, axis, [(i + 1, i) for i in range(count - 1)])
    return jnp.concatenate([before, cells, after], axis=dim)


def pinned(cells):
    return with_layout_constraint(cells, Layout(major_to_minor=tuple(range(cells.ndim))))


def inside_mask(axis, tile, width):
    count = lax.axis_size(axis)
    start = lax.axis_index(axis) * tile - width
    index = start + jnp.arange(tile + 2 * width, dtype=jnp.int32)
    return (index >= 0) & (index < count * tile)


def sweep(field, source, keep):
    diff_col = field[:-1, 1:] - field[:-1, :-1]
    diff_row = field[1:, :-1] - field[:-1, :-1]
    energy_sum = jnp.sum(diff_col * diff_col + diff_row * diff_row, axis=-1, keepdims=True)
    weight = 1.0 / jnp.sqrt(1.0 + energy_sum / field.shape[-1])
    flux_col = weight * diff_col
    flux_row = weight * diff_row
    spread = flux_col[1:, 1:] - flux_col[1:, :-1] + flux_row[1:, 1:] - flux_row[:-1, 1:]
    centre = field[1:-1, 1:-1]
    new = centre + tau_step * spread + tau_step * fidelity * (source - centre)
    return jnp.where(keep, new, 0.0)


def cholesky_qr(block):
    size = block.shape[1]
    inner = lax.dot_general(
        block, block, (((0,), (0,)), ((), ())),
        precision=lax.Precision.HIGHEST, preferred_element_type=jnp.float32,
    )
    sub = lax.broadcasted_iota(jnp.int32, (size, size), 0)
    lane = lax.broadcasted_iota(jnp.int32, (size, size), 1)
    upper = jnp.zeros((size, size), jnp.float32)
    inverse = jnp.zeros((size, size), jnp.float32)
    rest = inner
    for j in range(size):
        col = jnp.sum(jnp.where(lane == j, rest, 0.0), axis=1, keepdims=True)
        row = jnp.sum(jnp.where(sub == j, rest, 0.0), axis=0, keepdims=True)
        pivot = jnp.sqrt(jnp.sum(jnp.where(lane[:1] == j, row, 0.0), axis=1, keepdims=True))
        col = jnp.where(sub[:, :1] >= j, col / pivot, 0.0)
        row = jnp.where(lane[:1] >= j, row / pivot, 0.0)
        upper = upper + jnp.where(sub == j, row, 0.0)
        rest = rest - col * row
        coef = jnp.sum(jnp.where(lane == j, upper, 0.0), axis=1, keepdims=True)
        diag = jnp.sum(jnp.where(sub[:, :1] == j, coef, 0.0), axis=0, keepdims=True)
        acc = jnp.sum(jnp.where(sub[:, :1] < j, coef, 0.0) * inverse, axis=0, keepdims=True)
        unit = jnp.where(lane[:1] == j, 1.0, 0.0)
        inverse = inverse + jnp.where(sub == j, (unit - acc) / diag, 0.0)
    return lax.dot_general(
        block, inverse, (((1,), (1,)), ((), ())),
        precision=lax.Precision.HIGHEST, preferred_element_type=jnp.float32,
    )


def subspace_kernel(gram_ref, basis_ref, out_ref):
    product = jnp.dot(
        gram_ref[...], basis_ref[...],
        precision=lax.Precision.HIGHEST, preferred_element_type=jnp.float32,
    )
    out_ref[...] = cholesky_qr(cholesky_qr(product))


def subspace_step(gram_full, basis):
    return pl.pallas_call(
        subspace_kernel,
        out_shape=jax.ShapeDtypeStruct(basis.shape, jnp.float32),
        cost_estimate=pl.CostEstimate(
            flops=2 * gram_full.shape[0] * gram_full.size + 8 * basis.size * basis.shape[1],
            transcendentals=2 * basis.shape[1],
            bytes_accessed=4 * (gram_full.size + 2 * basis.size),
        ),
    )(gram_full, basis)


def orthonormal(block):
    inner = jnp.dot(block.T, block, precision=lax.Precision.HIGHEST)
    lower = jnp.linalg.cholesky(inner)
    return lax.linalg.triangular_solve(lower, block, left_side=False, lower=True, transpose_a=True)


def shards(order, image, start_basis):
    band_count, tile_rows, tile_cols = image.shape
    width = SWEEPS
    cells = pinned(jnp.transpose(image, (1, 2, 0)))
    ext = with_halo(cells, "row", 0, width)
    ext = with_halo(ext, "col", 1, width)
    row_in = inside_mask("row", tile_rows, width)
    col_in = inside_mask("col", tile_cols, width)
    field = ext
    for sweep_no in range(SWEEPS):
        left = width - sweep_no - 1
        lo = sweep_no + 1
        nr = tile_rows + 2 * left
        nc = tile_cols + 2 * left
        source = ext[lo:lo + nr, lo:lo + nc]
        keep = (row_in[lo:lo + nr, None] & col_in[None, lo:lo + nc])[:, :, None]
        field = pinned(sweep(field, source, keep))
    flat_cells = field.reshape(tile_rows * tile_cols, band_count)
    smoothed = jnp.transpose(field, (2, 0, 1))
    local_gram = lax.dot_general(
        flat_cells,
        flat_cells,
        (((0,), (0,)), ((), ())),
        precision=lax.Precision.HIGHEST,
        preferred_element_type=jnp.float32,
    )
    gram_full = paired_sum(local_gram, order)
    basis_now = start_basis
    for turn in range(SUBIT):
        basis_now = subspace_step(gram_full, basis_now)
    coeffs = jnp.dot(flat_cells, basis_now, precision=lax.Precision.HIGHEST)
    lowrank = lax.dot_general(
        basis_now,
        coeffs,
        (((1,), (1,)), ((), ())),
        precision=lax.Precision.HIGHEST,
    )
    return (smoothed, lowrank.reshape(band_count, tile_rows, tile_cols))


def solution(mesh):
    in_specs = (P(None, "row", "col"), P())
    out_specs = (P(None, "row", "col"), P(None, "row", "col"))
    body = functools.partial(shards, core_first(mesh))
    return jax.shard_map(body, mesh=mesh, in_specs=in_specs, out_specs=out_specs, check_vma=False)
```

```python
import functools

import jax
import jax.numpy as jnp
from jax import lax
from jax.sharding import PartitionSpec as P
from jax.experimental import pallas as pl
from jax.experimental.layout import Layout, with_layout_constraint
from jax.experimental.pallas import tpu as pltpu

SWEEPS = 4
SUBIT = 2


tau_step = 0.22
fidelity = 0.1


def butterfly_sum(value, axes, start=1):
    for axis in axes:
        count = lax.axis_size(axis)
        if count & (count - 1):
            value = lax.psum(value, axis)
            continue
        step = start if axis == axes[0] else 1
        while step < count:
            partner = lax.ppermute(value, axis, [(i, i ^ step) for i in range(count)])
            value = value + partner
            step *= 2
    return value


def paired_sum(value, axes):
    first = axes[0]
    count = lax.axis_size(first)
    half = value.shape[0] // 2
    if count < 2 or count & (count - 1) or value.shape[0] % 2:
        return butterfly_sum(value, axes)
    pairs = [(i, i ^ 1) for i in range(count)]
    low = lax.axis_index(first) % 2 == 0
    top, bottom = value[:half], value[half:]
    keep = jnp.where(low, top, bottom)
    give = jnp.where(low, bottom, top)
    part = keep + lax.ppermute(give, first, pairs)
    part = butterfly_sum(part, axes, start=2)
    other = lax.ppermute(part, first, pairs)
    return jnp.where(low, jnp.concatenate([part, other]), jnp.concatenate([other, part]))


def core_first(mesh):
    names = tuple(mesh.axis_names)
    devices = mesh.devices
    for pos, name in enumerate(names):
        if devices.shape[pos] < 2:
            continue
        at = [0] * devices.ndim
        one = devices[tuple(at)]
        at[pos] = 1
        two = devices[tuple(at)]
        coords = getattr(one, "coords", None)
        if coords is not None and tuple(coords) == tuple(getattr(two, "coords", ())):
            return (name,) + tuple(n for n in names if n != name)
    return names


def flat_permute(block, axis, pairs):
    pixels = block.size // block.shape[-1]
    if pixels % 64 or pixels <= block.shape[-1]:
        return lax.ppermute(block, axis, pairs)
    flat = block.reshape(pixels // 64, 64, block.shape[-1])
    return lax.ppermute(flat, axis, pairs).reshape(block.shape)


def with_halo(cells, axis, dim, width):
    count = lax.axis_size(axis)
    size = cells.shape[dim]
    head = lax.slice_in_dim(cells, 0, width, axis=dim)
    tail = lax.slice_in_dim(cells, size - width, size, axis=dim)
    before = flat_permute(tail, axis, [(i, i + 1) for i in range(count - 1)])
    after = flat_permute(head, axis, [(i + 1, i) for i in range(count - 1)])
    return jnp.concatenate([before, cells, after], axis=dim)


def pinned(cells):
    return with_layout_constraint(cells, Layout(major_to_minor=tuple(range(cells.ndim))))


def with_ring(cells, width):
    rows_n = lax.axis_size("row")
    cols_n = lax.axis_size("col")
    tile_rows, tile_cols = cells.shape[0], cells.shape[1]
    down = [(i, i + 1) for i in range(rows_n - 1)]
    up = [(i + 1, i) for i in range(rows_n - 1)]
    right = [(i, i + 1) for i in range(cols_n - 1)]
    left = [(i + 1, i) for i in range(cols_n - 1)]
    top = flat_permute(cells[tile_rows - width:], "row", down)
    bottom = flat_permute(cells[:width], "row", up)
    west = lax.ppermute(cells[:, tile_cols - width:], "col", right)
    east = lax.ppermute(cells[:, :width], "col", left)
    rims = jnp.concatenate([top, bottom], axis=0)
    rim_west = lax.ppermute(rims[:, tile_cols - width:], "col", right)
    rim_east = lax.ppermute(rims[:, :width], "col", left)
    return jnp.concatenate(
        [
            jnp.concatenate([rim_west[:width], top, rim_east[:width]], axis=1),
            jnp.concatenate([west, cells, east], axis=1),
            jnp.concatenate([rim_west[width:], bottom, rim_east[width:]], axis=1),
        ],
        axis=0,
    )


def inside_mask(axis, tile, width):
    count = lax.axis_size(axis)
    start = lax.axis_index(axis) * tile - width
    index = start + jnp.arange(tile + 2 * width, dtype=jnp.int32)
    return (index >= 0) & (index < count * tile)


def sweep(field, source, keep):
    diff_col = field[:-1, 1:] - field[:-1, :-1]
    diff_row = field[1:, :-1] - field[:-1, :-1]
    energy_sum = jnp.sum(diff_col * diff_col + diff_row * diff_row, axis=-1, keepdims=True)
    weight = 1.0 / jnp.sqrt(1.0 + energy_sum / field.shape[-1])
    flux_col = weight * diff_col
    flux_row = weight * diff_row
    spread = flux_col[1:, 1:] - flux_col[1:, :-1] + flux_row[1:, 1:] - flux_row[:-1, 1:]
    centre = field[1:-1, 1:-1]
    new = centre + tau_step * spread + tau_step * fidelity * (source - centre)
    return jnp.where(keep, new, 0.0)


def cholesky_qr(block):
    size = block.shape[1]
    inner = lax.dot_general(
        block, block, (((0,), (0,)), ((), ())),
        precision=lax.Precision.HIGHEST, preferred_element_type=jnp.float32,
    )
    sub = lax.broadcasted_iota(jnp.int32, (size, size), 0)
    lane = lax.broadcasted_iota(jnp.int32, (size, size), 1)
    upper = jnp.zeros((size, size), jnp.float32)
    inverse = jnp.zeros((size, size), jnp.float32)
    rest = inner
    for j in range(size):
        col = jnp.sum(jnp.where(lane == j, rest, 0.0), axis=1, keepdims=True)
        row = jnp.sum(jnp.where(sub == j, rest, 0.0), axis=0, keepdims=True)
        pivot = jnp.sqrt(jnp.sum(jnp.where(lane[:1] == j, row, 0.0), axis=1, keepdims=True))
        col = jnp.where(sub[:, :1] >= j, col / pivot, 0.0)
        row = jnp.where(lane[:1] >= j, row / pivot, 0.0)
        upper = upper + jnp.where(sub == j, row, 0.0)
        rest = rest - col * row
        coef = jnp.sum(jnp.where(lane == j, upper, 0.0), axis=1, keepdims=True)
        diag = jnp.sum(jnp.where(sub[:, :1] == j, coef, 0.0), axis=0, keepdims=True)
        acc = jnp.sum(jnp.where(sub[:, :1] < j, coef, 0.0) * inverse, axis=0, keepdims=True)
        unit = jnp.where(lane[:1] == j, 1.0, 0.0)
        inverse = inverse + jnp.where(sub == j, (unit - acc) / diag, 0.0)
    return lax.dot_general(
        block, inverse, (((1,), (1,)), ((), ())),
        precision=lax.Precision.HIGHEST, preferred_element_type=jnp.float32,
    )


def subspace_kernel(gram_ref, basis_ref, out_ref):
    product = jnp.dot(
        gram_ref[...], basis_ref[...],
        precision=lax.Precision.HIGHEST, preferred_element_type=jnp.float32,
    )
    out_ref[...] = cholesky_qr(cholesky_qr(product))


def subspace_step(gram_full, basis):
    return pl.pallas_call(
        subspace_kernel,
        out_shape=jax.ShapeDtypeStruct(basis.shape, jnp.float32),
        cost_estimate=pl.CostEstimate(
            flops=2 * gram_full.shape[0] * gram_full.size + 8 * basis.size * basis.shape[1],
            transcendentals=2 * basis.shape[1],
            bytes_accessed=4 * (gram_full.size + 2 * basis.size),
        ),
    )(gram_full, basis)


def orthonormal(block):
    inner = jnp.dot(block.T, block, precision=lax.Precision.HIGHEST)
    lower = jnp.linalg.cholesky(inner)
    return lax.linalg.triangular_solve(lower, block, left_side=False, lower=True, transpose_a=True)


def shards(order, image, start_basis):
    band_count, tile_rows, tile_cols = image.shape
    width = SWEEPS
    cells = pinned(jnp.transpose(image, (1, 2, 0)))
    ext = with_ring(cells, width)
    row_in = inside_mask("row", tile_rows, width)
    col_in = inside_mask("col", tile_cols, width)
    field = ext
    for sweep_no in range(SWEEPS):
        left = width - sweep_no - 1
        lo = sweep_no + 1
        nr = tile_rows + 2 * left
        nc = tile_cols + 2 * left
        source = ext[lo:lo + nr, lo:lo + nc]
        keep = (row_in[lo:lo + nr, None] & col_in[None, lo:lo + nc])[:, :, None]
        field = pinned(sweep(field, source, keep))
    flat_cells = field.reshape(tile_rows * tile_cols, band_count)
    smoothed = jnp.transpose(field, (2, 0, 1))
    local_gram = lax.dot_general(
        flat_cells,
        flat_cells,
        (((0,), (0,)), ((), ())),
        precision=lax.Precision.HIGHEST,
        preferred_element_type=jnp.float32,
    )
    gram_full = paired_sum(local_gram, order)
    basis_now = start_basis
    for turn in range(SUBIT):
        basis_now = subspace_step(gram_full, basis_now)
    coeffs = jnp.dot(flat_cells, basis_now, precision=lax.Precision.HIGHEST)
    lowrank = lax.dot_general(
        basis_now,
        coeffs,
        (((1,), (1,)), ((), ())),
        precision=lax.Precision.HIGHEST,
    )
    return (smoothed, lowrank.reshape(band_count, tile_rows, tile_cols))


def solution(mesh):
    in_specs = (P(None, "row", "col"), P())
    out_specs = (P(None, "row", "col"), P(None, "row", "col"))
    body = functools.partial(shards, core_first(mesh))
    return jax.shard_map(body, mesh=mesh, in_specs=in_specs, out_specs=out_specs, check_vma=False)
```

```python
import functools

import jax
import jax.numpy as jnp
from jax import lax
from jax.sharding import PartitionSpec as P
from jax.experimental import pallas as pl
from jax.experimental.layout import Layout, with_layout_constraint
from jax.experimental.pallas import tpu as pltpu

SWEEPS = 4
SUBIT = 2


tau_step = 0.22
fidelity = 0.1


def butterfly_sum(value, axes, start=1):
    for axis in axes:
        count = lax.axis_size(axis)
        if count & (count - 1):
            value = lax.psum(value, axis)
            continue
        step = start if axis == axes[0] else 1
        while step < count:
            partner = lax.ppermute(value, axis, [(i, i ^ step) for i in range(count)])
            value = value + partner
            step *= 2
    return value


def paired_sum(value, axes):
    first = axes[0]
    count = lax.axis_size(first)
    half = value.shape[0] // 2
    if count < 2 or count & (count - 1) or value.shape[0] % 2:
        return butterfly_sum(value, axes)
    pairs = [(i, i ^ 1) for i in range(count)]
    low = lax.axis_index(first) % 2 == 0
    top, bottom = value[:half], value[half:]
    keep = jnp.where(low, top, bottom)
    give = jnp.where(low, bottom, top)
    part = keep + lax.ppermute(give, first, pairs)
    part = butterfly_sum(part, axes, start=2)
    other = lax.ppermute(part, first, pairs)
    return jnp.where(low, jnp.concatenate([part, other]), jnp.concatenate([other, part]))


def core_first(mesh):
    names = tuple(mesh.axis_names)
    devices = mesh.devices
    for pos, name in enumerate(names):
        if devices.shape[pos] < 2:
            continue
        at = [0] * devices.ndim
        one = devices[tuple(at)]
        at[pos] = 1
        two = devices[tuple(at)]
        coords = getattr(one, "coords", None)
        if coords is not None and tuple(coords) == tuple(getattr(two, "coords", ())):
            return (name,) + tuple(n for n in names if n != name)
    return names


def flat_permute(block, axis, pairs):
    pixels = block.size // block.shape[-1]
    if pixels % 64 or pixels <= block.shape[-1]:
        return lax.ppermute(block, axis, pairs)
    flat = block.reshape(pixels // 64, 64, block.shape[-1])
    return lax.ppermute(flat, axis, pairs).reshape(block.shape)


def with_halo(cells, axis, dim, width):
    count = lax.axis_size(axis)
    size = cells.shape[dim]
    head = lax.slice_in_dim(cells, 0, width, axis=dim)
    tail = lax.slice_in_dim(cells, size - width, size, axis=dim)
    before = flat_permute(tail, axis, [(i, i + 1) for i in range(count - 1)])
    after = flat_permute(head, axis, [(i + 1, i) for i in range(count - 1)])
    return jnp.concatenate([before, cells, after], axis=dim)


def pinned(cells):
    return with_layout_constraint(cells, Layout(major_to_minor=tuple(range(cells.ndim))))


def with_ring(cells, width):
    rows_n = lax.axis_size("row")
    cols_n = lax.axis_size("col")
    tile_rows, tile_cols = cells.shape[0], cells.shape[1]
    down = [(i, i + 1) for i in range(rows_n - 1)]
    up = [(i + 1, i) for i in range(rows_n - 1)]
    right = [(i, i + 1) for i in range(cols_n - 1)]
    left = [(i + 1, i) for i in range(cols_n - 1)]
    top = flat_permute(cells[tile_rows - width:], "row", down)
    bottom = flat_permute(cells[:width], "row", up)
    west = lax.ppermute(cells[:, tile_cols - width:], "col", right)
    east = lax.ppermute(cells[:, :width], "col", left)
    rims = jnp.concatenate([top, bottom], axis=0)
    rim_west = lax.ppermute(rims[:, tile_cols - width:], "col", right)
    rim_east = lax.ppermute(rims[:, :width], "col", left)
    return jnp.concatenate(
        [
            jnp.concatenate([rim_west[:width], top, rim_east[:width]], axis=1),
            jnp.concatenate([west, cells, east], axis=1),
            jnp.concatenate([rim_west[width:], bottom, rim_east[width:]], axis=1),
        ],
        axis=0,
    )


def inside_mask(axis, tile, width):
    count = lax.axis_size(axis)
    start = lax.axis_index(axis) * tile - width
    index = start + jnp.arange(tile + 2 * width, dtype=jnp.int32)
    return (index >= 0) & (index < count * tile)


def sweep(field, source, keep):
    diff_col = field[:-1, 1:] - field[:-1, :-1]
    diff_row = field[1:, :-1] - field[:-1, :-1]
    energy_sum = jnp.sum(diff_col * diff_col + diff_row * diff_row, axis=-1, keepdims=True)
    weight = 1.0 / jnp.sqrt(1.0 + energy_sum / field.shape[-1])
    flux_col = weight * diff_col
    flux_row = weight * diff_row
    spread = flux_col[1:, 1:] - flux_col[1:, :-1] + flux_row[1:, 1:] - flux_row[:-1, 1:]
    centre = field[1:-1, 1:-1]
    new = centre + tau_step * spread + tau_step * fidelity * (source - centre)
    return jnp.where(keep, new, 0.0)


def cholesky_qr(block):
    size = block.shape[1]
    inner = lax.dot_general(
        block, block, (((0,), (0,)), ((), ())),
        precision=lax.Precision.HIGHEST, preferred_element_type=jnp.float32,
    )
    sub = lax.broadcasted_iota(jnp.int32, (size, size), 0)
    lane = lax.broadcasted_iota(jnp.int32, (size, size), 1)
    upper = jnp.zeros((size, size), jnp.float32)
    inverse = jnp.zeros((size, size), jnp.float32)
    rest = inner
    for j in range(size):
        col = rest[:, j:j + 1]
        row = rest[j:j + 1, :]
        pivot = jnp.sqrt(rest[j:j + 1, j:j + 1])
        col = jnp.where(sub[:, :1] >= j, col / pivot, 0.0)
        row = jnp.where(lane[:1] >= j, row / pivot, 0.0)
        upper = upper + jnp.where(sub == j, row, 0.0)
        rest = rest - col * row
        coef = upper[:, j:j + 1]
        diag = upper[j:j + 1, j:j + 1]
        acc = jnp.sum(jnp.where(sub[:, :1] < j, coef, 0.0) * inverse, axis=0, keepdims=True)
        unit = jnp.where(lane[:1] == j, 1.0, 0.0)
        inverse = inverse + jnp.where(sub == j, (unit - acc) / diag, 0.0)
    return lax.dot_general(
        block, inverse, (((1,), (1,)), ((), ())),
        precision=lax.Precision.HIGHEST, preferred_element_type=jnp.float32,
    )


def subspace_kernel(gram_ref, basis_ref, out_ref):
    product = jnp.dot(
        gram_ref[...], basis_ref[...],
        precision=lax.Precision.HIGHEST, preferred_element_type=jnp.float32,
    )
    out_ref[...] = cholesky_qr(cholesky_qr(product))


def subspace_step(gram_full, basis):
    return pl.pallas_call(
        subspace_kernel,
        out_shape=jax.ShapeDtypeStruct(basis.shape, jnp.float32),
        cost_estimate=pl.CostEstimate(
            flops=2 * gram_full.shape[0] * gram_full.size + 8 * basis.size * basis.shape[1],
            transcendentals=2 * basis.shape[1],
            bytes_accessed=4 * (gram_full.size + 2 * basis.size),
        ),
    )(gram_full, basis)


def orthonormal(block):
    inner = jnp.dot(block.T, block, precision=lax.Precision.HIGHEST)
    lower = jnp.linalg.cholesky(inner)
    return lax.linalg.triangular_solve(lower, block, left_side=False, lower=True, transpose_a=True)


def shards(order, image, start_basis):
    band_count, tile_rows, tile_cols = image.shape
    width = SWEEPS
    cells = pinned(jnp.transpose(image, (1, 2, 0)))
    ext = with_ring(cells, width)
    row_in = inside_mask("row", tile_rows, width)
    col_in = inside_mask("col", tile_cols, width)
    field = ext
    for sweep_no in range(SWEEPS):
        left = width - sweep_no - 1
        lo = sweep_no + 1
        nr = tile_rows + 2 * left
        nc = tile_cols + 2 * left
        source = ext[lo:lo + nr, lo:lo + nc]
        keep = (row_in[lo:lo + nr, None] & col_in[None, lo:lo + nc])[:, :, None]
        field = pinned(sweep(field, source, keep))
    flat_cells = field.reshape(tile_rows * tile_cols, band_count)
    smoothed = jnp.transpose(field, (2, 0, 1))
    local_gram = lax.dot_general(
        flat_cells,
        flat_cells,
        (((0,), (0,)), ((), ())),
        precision=lax.Precision.HIGHEST,
        preferred_element_type=jnp.float32,
    )
    gram_full = paired_sum(local_gram, order)
    basis_now = start_basis
    for turn in range(SUBIT):
        basis_now = subspace_step(gram_full, basis_now)
    coeffs = jnp.dot(flat_cells, basis_now, precision=lax.Precision.HIGHEST)
    lowrank = lax.dot_general(
        basis_now,
        coeffs,
        (((1,), (1,)), ((), ())),
        precision=lax.Precision.HIGHEST,
    )
    return (smoothed, lowrank.reshape(band_count, tile_rows, tile_cols))


def solution(mesh):
    in_specs = (P(None, "row", "col"), P())
    out_specs = (P(None, "row", "col"), P(None, "row", "col"))
    body = functools.partial(shards, core_first(mesh))
    return jax.shard_map(body, mesh=mesh, in_specs=in_specs, out_specs=out_specs, check_vma=False)
```

```python
import functools

import jax
import jax.numpy as jnp
from jax import lax
from jax.sharding import PartitionSpec as P
from jax.experimental import pallas as pl
from jax.experimental.layout import Layout, with_layout_constraint
from jax.experimental.pallas import tpu as pltpu

SWEEPS = 4
SUBIT = 2


tau_step = 0.22
fidelity = 0.1


def butterfly_sum(value, axes, start=1):
    for axis in axes:
        count = lax.axis_size(axis)
        if count & (count - 1):
            value = lax.psum(value, axis)
            continue
        step = start if axis == axes[0] else 1
        while step < count:
            partner = lax.ppermute(value, axis, [(i, i ^ step) for i in range(count)])
            value = value + partner
            step *= 2
    return value


def paired_sum(value, axes):
    first = axes[0]
    count = lax.axis_size(first)
    half = value.shape[0] // 2
    if count < 2 or count & (count - 1) or value.shape[0] % 2:
        return butterfly_sum(value, axes)
    pairs = [(i, i ^ 1) for i in range(count)]
    low = lax.axis_index(first) % 2 == 0
    top, bottom = value[:half], value[half:]
    keep = jnp.where(low, top, bottom)
    give = jnp.where(low, bottom, top)
    part = keep + lax.ppermute(give, first, pairs)
    part = butterfly_sum(part, axes, start=2)
    other = lax.ppermute(part, first, pairs)
    return jnp.where(low, jnp.concatenate([part, other]), jnp.concatenate([other, part]))


def core_first(mesh):
    names = tuple(mesh.axis_names)
    devices = mesh.devices
    for pos, name in enumerate(names):
        if devices.shape[pos] < 2:
            continue
        at = [0] * devices.ndim
        one = devices[tuple(at)]
        at[pos] = 1
        two = devices[tuple(at)]
        coords = getattr(one, "coords", None)
        if coords is not None and tuple(coords) == tuple(getattr(two, "coords", ())):
            return (name,) + tuple(n for n in names if n != name)
    return names


def flat_permute(block, axis, pairs):
    pixels = block.size // block.shape[-1]
    if pixels % 64 or pixels <= block.shape[-1]:
        return lax.ppermute(block, axis, pairs)
    flat = block.reshape(pixels // 64, 64, block.shape[-1])
    return lax.ppermute(flat, axis, pairs).reshape(block.shape)


def with_halo(cells, axis, dim, width):
    count = lax.axis_size(axis)
    size = cells.shape[dim]
    head = lax.slice_in_dim(cells, 0, width, axis=dim)
    tail = lax.slice_in_dim(cells, size - width, size, axis=dim)
    before = flat_permute(tail, axis, [(i, i + 1) for i in range(count - 1)])
    after = flat_permute(head, axis, [(i + 1, i) for i in range(count - 1)])
    return jnp.concatenate([before, cells, after], axis=dim)


def pinned(cells):
    return with_layout_constraint(cells, Layout(major_to_minor=tuple(range(cells.ndim))))


def with_ring(cells, width):
    rows_n = lax.axis_size("row")
    cols_n = lax.axis_size("col")
    tile_rows, tile_cols = cells.shape[0], cells.shape[1]
    down = [(i, i + 1) for i in range(rows_n - 1)]
    up = [(i + 1, i) for i in range(rows_n - 1)]
    right = [(i, i + 1) for i in range(cols_n - 1)]
    left = [(i + 1, i) for i in range(cols_n - 1)]
    top = flat_permute(cells[tile_rows - width:], "row", down)
    bottom = flat_permute(cells[:width], "row", up)
    west = lax.ppermute(cells[:, tile_cols - width:], "col", right)
    east = lax.ppermute(cells[:, :width], "col", left)
    rims = jnp.concatenate([top, bottom], axis=0)
    rim_west = lax.ppermute(rims[:, tile_cols - width:], "col", right)
    rim_east = lax.ppermute(rims[:, :width], "col", left)
    return jnp.concatenate(
        [
            jnp.concatenate([rim_west[:width], top, rim_east[:width]], axis=1),
            jnp.concatenate([west, cells, east], axis=1),
            jnp.concatenate([rim_west[width:], bottom, rim_east[width:]], axis=1),
        ],
        axis=0,
    )


def inside_mask(axis, tile, width):
    count = lax.axis_size(axis)
    start = lax.axis_index(axis) * tile - width
    index = start + jnp.arange(tile + 2 * width, dtype=jnp.int32)
    return (index >= 0) & (index < count * tile)


def sweep(field, source, keep):
    diff_col = field[:-1, 1:] - field[:-1, :-1]
    diff_row = field[1:, :-1] - field[:-1, :-1]
    energy_sum = jnp.sum(diff_col * diff_col + diff_row * diff_row, axis=-1, keepdims=True)
    weight = 1.0 / jnp.sqrt(1.0 + energy_sum / field.shape[-1])
    flux_col = weight * diff_col
    flux_row = weight * diff_row
    spread = flux_col[1:, 1:] - flux_col[1:, :-1] + flux_row[1:, 1:] - flux_row[:-1, 1:]
    centre = field[1:-1, 1:-1]
    new = centre + tau_step * spread + tau_step * fidelity * (source - centre)
    return jnp.where(keep, new, 0.0)


def cholesky_qr(block):
    size = block.shape[1]
    inner = lax.dot_general(
        block, block, (((0,), (0,)), ((), ())),
        precision=lax.Precision.HIGHEST, preferred_element_type=jnp.float32,
    )
    sub = lax.broadcasted_iota(jnp.int32, (size, size), 0)
    lane = lax.broadcasted_iota(jnp.int32, (size, size), 1)
    upper = jnp.zeros((size, size), jnp.float32)
    inverse = jnp.zeros((size, size), jnp.float32)
    rest = inner
    for j in range(size):
        col = rest[:, j:j + 1]
        row = rest[j:j + 1, :]
        pivot = jnp.sqrt(rest[j:j + 1, j:j + 1])
        col = jnp.where(sub[:, :1] >= j, col / pivot, 0.0)
        row = jnp.where(lane[:1] >= j, row / pivot, 0.0)
        upper = upper + jnp.where(sub == j, row, 0.0)
        rest = rest - col * row
        coef = upper[:, j:j + 1]
        diag = upper[j:j + 1, j:j + 1]
        acc = jnp.sum(jnp.where(sub[:, :1] < j, coef, 0.0) * inverse, axis=0, keepdims=True)
        unit = jnp.where(lane[:1] == j, 1.0, 0.0)
        inverse = inverse + jnp.where(sub == j, (unit - acc) / diag, 0.0)
    return lax.dot_general(
        block, inverse, (((1,), (1,)), ((), ())),
        precision=lax.Precision.HIGHEST, preferred_element_type=jnp.float32,
    )


def subspace_kernel(gram_ref, basis_ref, out_ref):
    basis = basis_ref[...]
    for turn in range(SUBIT):
        product = jnp.dot(
            gram_ref[...], basis,
            precision=lax.Precision.HIGHEST, preferred_element_type=jnp.float32,
        )
        basis = cholesky_qr(cholesky_qr(product))
    out_ref[...] = basis


def subspace_step(gram_full, basis):
    return pl.pallas_call(
        subspace_kernel,
        out_shape=jax.ShapeDtypeStruct(basis.shape, jnp.float32),
        cost_estimate=pl.CostEstimate(
            flops=SUBIT * (2 * gram_full.shape[0] * gram_full.size + 8 * basis.size * basis.shape[1]),
            transcendentals=SUBIT * 2 * basis.shape[1],
            bytes_accessed=4 * (gram_full.size + 2 * basis.size),
        ),
    )(gram_full, basis)


def orthonormal(block):
    inner = jnp.dot(block.T, block, precision=lax.Precision.HIGHEST)
    lower = jnp.linalg.cholesky(inner)
    return lax.linalg.triangular_solve(lower, block, left_side=False, lower=True, transpose_a=True)


def shards(order, image, start_basis):
    band_count, tile_rows, tile_cols = image.shape
    width = SWEEPS
    cells = pinned(jnp.transpose(image, (1, 2, 0)))
    ext = with_ring(cells, width)
    row_in = inside_mask("row", tile_rows, width)
    col_in = inside_mask("col", tile_cols, width)
    field = ext
    for sweep_no in range(SWEEPS):
        left = width - sweep_no - 1
        lo = sweep_no + 1
        nr = tile_rows + 2 * left
        nc = tile_cols + 2 * left
        source = ext[lo:lo + nr, lo:lo + nc]
        keep = (row_in[lo:lo + nr, None] & col_in[None, lo:lo + nc])[:, :, None]
        field = pinned(sweep(field, source, keep))
    flat_cells = field.reshape(tile_rows * tile_cols, band_count)
    smoothed = jnp.transpose(field, (2, 0, 1))
    local_gram = lax.dot_general(
        flat_cells,
        flat_cells,
        (((0,), (0,)), ((), ())),
        precision=lax.Precision.HIGHEST,
        preferred_element_type=jnp.float32,
    )
    gram_full = paired_sum(local_gram, order)
    basis_now = start_basis
    basis_now = subspace_step(gram_full, basis_now)
    coeffs = jnp.dot(flat_cells, basis_now, precision=lax.Precision.HIGHEST)
    lowrank = lax.dot_general(
        basis_now,
        coeffs,
        (((1,), (1,)), ((), ())),
        precision=lax.Precision.HIGHEST,
    )
    return (smoothed, lowrank.reshape(band_count, tile_rows, tile_cols))


def solution(mesh):
    in_specs = (P(None, "row", "col"), P())
    out_specs = (P(None, "row", "col"), P(None, "row", "col"))
    body = functools.partial(shards, core_first(mesh))
    return jax.shard_map(body, mesh=mesh, in_specs=in_specs, out_specs=out_specs, check_vma=False)
```

```python
import functools

import jax
import jax.numpy as jnp
from jax import lax
from jax.sharding import PartitionSpec as P
from jax.experimental import pallas as pl
from jax.experimental.layout import Layout, with_layout_constraint
from jax.experimental.pallas import tpu as pltpu

SWEEPS = 4
SUBIT = 2


tau_step = 0.22
fidelity = 0.1


def butterfly_sum(value, axes, start=1):
    for axis in axes:
        count = lax.axis_size(axis)
        if count & (count - 1):
            value = lax.psum(value, axis)
            continue
        step = start if axis == axes[0] else 1
        while step < count:
            partner = lax.ppermute(value, axis, [(i, i ^ step) for i in range(count)])
            value = value + partner
            step *= 2
    return value


def paired_sum(value, axes):
    first = axes[0]
    count = lax.axis_size(first)
    half = value.shape[0] // 2
    if count < 2 or count & (count - 1) or value.shape[0] % 2:
        return butterfly_sum(value, axes)
    pairs = [(i, i ^ 1) for i in range(count)]
    low = lax.axis_index(first) % 2 == 0
    top, bottom = value[:half], value[half:]
    keep = jnp.where(low, top, bottom)
    give = jnp.where(low, bottom, top)
    part = keep + lax.ppermute(give, first, pairs)
    part = butterfly_sum(part, axes, start=2)
    other = lax.ppermute(part, first, pairs)
    return jnp.where(low, jnp.concatenate([part, other]), jnp.concatenate([other, part]))


def core_first(mesh):
    names = tuple(mesh.axis_names)
    devices = mesh.devices
    for pos, name in enumerate(names):
        if devices.shape[pos] < 2:
            continue
        at = [0] * devices.ndim
        one = devices[tuple(at)]
        at[pos] = 1
        two = devices[tuple(at)]
        coords = getattr(one, "coords", None)
        if coords is not None and tuple(coords) == tuple(getattr(two, "coords", ())):
            return (name,) + tuple(n for n in names if n != name)
    return names


def flat_permute(block, axis, pairs):
    pixels = block.size // block.shape[-1]
    if pixels % 64 or pixels <= block.shape[-1]:
        return lax.ppermute(block, axis, pairs)
    flat = block.reshape(pixels // 64, 64, block.shape[-1])
    return lax.ppermute(flat, axis, pairs).reshape(block.shape)


def grouped_permute(block, axis, pairs):
    bands, rows, cols = block.shape
    group = 1
    while bands % (group * 2) == 0 and bands // (group * 2) >= group * 2 * rows:
        group *= 2
    flat = block.reshape(bands // group, group * rows, cols)
    return lax.ppermute(flat, axis, pairs).reshape(block.shape)


def with_halo(cells, axis, dim, width):
    count = lax.axis_size(axis)
    size = cells.shape[dim]
    head = lax.slice_in_dim(cells, 0, width, axis=dim)
    tail = lax.slice_in_dim(cells, size - width, size, axis=dim)
    before = flat_permute(tail, axis, [(i, i + 1) for i in range(count - 1)])
    after = flat_permute(head, axis, [(i + 1, i) for i in range(count - 1)])
    return jnp.concatenate([before, cells, after], axis=dim)


def pinned(cells):
    return with_layout_constraint(cells, Layout(major_to_minor=tuple(range(cells.ndim))))


def with_ring(cells, width, top, bottom):
    rows_n = lax.axis_size("row")
    cols_n = lax.axis_size("col")
    tile_rows, tile_cols = cells.shape[0], cells.shape[1]
    down = [(i, i + 1) for i in range(rows_n - 1)]
    up = [(i + 1, i) for i in range(rows_n - 1)]
    right = [(i, i + 1) for i in range(cols_n - 1)]
    left = [(i + 1, i) for i in range(cols_n - 1)]
    west = lax.ppermute(cells[:, tile_cols - width:], "col", right)
    east = lax.ppermute(cells[:, :width], "col", left)
    rims = jnp.concatenate([top, bottom], axis=0)
    rim_west = lax.ppermute(rims[:, tile_cols - width:], "col", right)
    rim_east = lax.ppermute(rims[:, :width], "col", left)
    return jnp.concatenate(
        [
            jnp.concatenate([rim_west[:width], top, rim_east[:width]], axis=1),
            jnp.concatenate([west, cells, east], axis=1),
            jnp.concatenate([rim_west[width:], bottom, rim_east[width:]], axis=1),
        ],
        axis=0,
    )


def inside_mask(axis, tile, width):
    count = lax.axis_size(axis)
    start = lax.axis_index(axis) * tile - width
    index = start + jnp.arange(tile + 2 * width, dtype=jnp.int32)
    return (index >= 0) & (index < count * tile)


def sweep(field, source, keep):
    diff_col = field[:-1, 1:] - field[:-1, :-1]
    diff_row = field[1:, :-1] - field[:-1, :-1]
    energy_sum = jnp.sum(diff_col * diff_col + diff_row * diff_row, axis=-1, keepdims=True)
    weight = 1.0 / jnp.sqrt(1.0 + energy_sum / field.shape[-1])
    flux_col = weight * diff_col
    flux_row = weight * diff_row
    spread = flux_col[1:, 1:] - flux_col[1:, :-1] + flux_row[1:, 1:] - flux_row[:-1, 1:]
    centre = field[1:-1, 1:-1]
    new = centre + tau_step * spread + tau_step * fidelity * (source - centre)
    return jnp.where(keep, new, 0.0)


def cholesky_qr(block):
    size = block.shape[1]
    inner = lax.dot_general(
        block, block, (((0,), (0,)), ((), ())),
        precision=lax.Precision.HIGHEST, preferred_element_type=jnp.float32,
    )
    sub = lax.broadcasted_iota(jnp.int32, (size, size), 0)
    lane = lax.broadcasted_iota(jnp.int32, (size, size), 1)
    upper = jnp.zeros((size, size), jnp.float32)
    inverse = jnp.zeros((size, size), jnp.float32)
    rest = inner
    for j in range(size):
        col = rest[:, j:j + 1]
        row = rest[j:j + 1, :]
        pivot = jnp.sqrt(rest[j:j + 1, j:j + 1])
        col = jnp.where(sub[:, :1] >= j, col / pivot, 0.0)
        row = jnp.where(lane[:1] >= j, row / pivot, 0.0)
        upper = upper + jnp.where(sub == j, row, 0.0)
        rest = rest - col * row
        coef = upper[:, j:j + 1]
        diag = upper[j:j + 1, j:j + 1]
        acc = jnp.sum(jnp.where(sub[:, :1] < j, coef, 0.0) * inverse, axis=0, keepdims=True)
        unit = jnp.where(lane[:1] == j, 1.0, 0.0)
        inverse = inverse + jnp.where(sub == j, (unit - acc) / diag, 0.0)
    return lax.dot_general(
        block, inverse, (((1,), (1,)), ((), ())),
        precision=lax.Precision.HIGHEST, preferred_element_type=jnp.float32,
    )


def subspace_kernel(gram_ref, basis_ref, out_ref):
    basis = basis_ref[...]
    for turn in range(SUBIT):
        product = jnp.dot(
            gram_ref[...], basis,
            precision=lax.Precision.HIGHEST, preferred_element_type=jnp.float32,
        )
        basis = cholesky_qr(cholesky_qr(product))
    out_ref[...] = basis


def subspace_step(gram_full, basis):
    return pl.pallas_call(
        subspace_kernel,
        out_shape=jax.ShapeDtypeStruct(basis.shape, jnp.float32),
        cost_estimate=pl.CostEstimate(
            flops=SUBIT * (2 * gram_full.shape[0] * gram_full.size + 8 * basis.size * basis.shape[1]),
            transcendentals=SUBIT * 2 * basis.shape[1],
            bytes_accessed=4 * (gram_full.size + 2 * basis.size),
        ),
    )(gram_full, basis)


def orthonormal(block):
    inner = jnp.dot(block.T, block, precision=lax.Precision.HIGHEST)
    lower = jnp.linalg.cholesky(inner)
    return lax.linalg.triangular_solve(lower, block, left_side=False, lower=True, transpose_a=True)


def shards(order, image, start_basis):
    band_count, tile_rows, tile_cols = image.shape
    width = SWEEPS
    down = [(i, i + 1) for i in range(lax.axis_size("row") - 1)]
    up = [(i + 1, i) for i in range(lax.axis_size("row") - 1)]
    top = grouped_permute(image[:, tile_rows - width:], "row", down)
    bottom = grouped_permute(image[:, :width], "row", up)
    cells = pinned(jnp.transpose(image, (1, 2, 0)))
    ext = with_ring(
        cells, width,
        pinned(jnp.transpose(top, (1, 2, 0))),
        pinned(jnp.transpose(bottom, (1, 2, 0))),
    )
    row_in = inside_mask("row", tile_rows, width)
    col_in = inside_mask("col", tile_cols, width)
    field = ext
    for sweep_no in range(SWEEPS):
        left = width - sweep_no - 1
        lo = sweep_no + 1
        nr = tile_rows + 2 * left
        nc = tile_cols + 2 * left
        source = ext[lo:lo + nr, lo:lo + nc]
        keep = (row_in[lo:lo + nr, None] & col_in[None, lo:lo + nc])[:, :, None]
        field = pinned(sweep(field, source, keep))
    flat_cells = field.reshape(tile_rows * tile_cols, band_count)
    smoothed = jnp.transpose(field, (2, 0, 1))
    local_gram = lax.dot_general(
        flat_cells,
        flat_cells,
        (((0,), (0,)), ((), ())),
        precision=lax.Precision.HIGHEST,
        preferred_element_type=jnp.float32,
    )
    gram_full = paired_sum(local_gram, order)
    basis_now = start_basis
    basis_now = subspace_step(gram_full, basis_now)
    coeffs = jnp.dot(flat_cells, basis_now, precision=lax.Precision.HIGHEST)
    lowrank = lax.dot_general(
        basis_now,
        coeffs,
        (((1,), (1,)), ((), ())),
        precision=lax.Precision.HIGHEST,
    )
    return (smoothed, lowrank.reshape(band_count, tile_rows, tile_cols))


def solution(mesh):
    in_specs = (P(None, "row", "col"), P())
    out_specs = (P(None, "row", "col"), P(None, "row", "col"))
    body = functools.partial(shards, core_first(mesh))
    return jax.shard_map(body, mesh=mesh, in_specs=in_specs, out_specs=out_specs, check_vma=False)
```

```python
import functools

import jax
import jax.numpy as jnp
from jax import lax
from jax.sharding import PartitionSpec as P
from jax.experimental import pallas as pl
from jax.experimental.layout import Layout, with_layout_constraint
from jax.experimental.pallas import tpu as pltpu

SWEEPS = 4
SUBIT = 2


tau_step = 0.22
fidelity = 0.1


def butterfly_sum(value, axes, start=1):
    for axis in axes:
        count = lax.axis_size(axis)
        if count & (count - 1):
            value = lax.psum(value, axis)
            continue
        step = start if axis == axes[0] else 1
        while step < count:
            partner = lax.ppermute(value, axis, [(i, i ^ step) for i in range(count)])
            value = value + partner
            step *= 2
    return value


def paired_sum(value, axes):
    first = axes[0]
    count = lax.axis_size(first)
    half = value.shape[0] // 2
    if count < 2 or count & (count - 1) or value.shape[0] % 2:
        return butterfly_sum(value, axes)
    pairs = [(i, i ^ 1) for i in range(count)]
    low = lax.axis_index(first) % 2 == 0
    top, bottom = value[:half], value[half:]
    keep = jnp.where(low, top, bottom)
    give = jnp.where(low, bottom, top)
    part = keep + lax.ppermute(give, first, pairs)
    part = butterfly_sum(part, axes, start=2)
    other = lax.ppermute(part, first, pairs)
    return jnp.where(low, jnp.concatenate([part, other]), jnp.concatenate([other, part]))


def core_first(mesh):
    names = tuple(mesh.axis_names)
    devices = mesh.devices
    for pos, name in enumerate(names):
        if devices.shape[pos] < 2:
            continue
        at = [0] * devices.ndim
        one = devices[tuple(at)]
        at[pos] = 1
        two = devices[tuple(at)]
        coords = getattr(one, "coords", None)
        if coords is not None and tuple(coords) == tuple(getattr(two, "coords", ())):
            return (name,) + tuple(n for n in names if n != name)
    return names


def flat_permute(block, axis, pairs):
    pixels = block.size // block.shape[-1]
    if pixels % 64 or pixels <= block.shape[-1]:
        return lax.ppermute(block, axis, pairs)
    flat = block.reshape(pixels // 64, 64, block.shape[-1])
    return lax.ppermute(flat, axis, pairs).reshape(block.shape)


def with_halo(cells, axis, dim, width):
    count = lax.axis_size(axis)
    size = cells.shape[dim]
    head = lax.slice_in_dim(cells, 0, width, axis=dim)
    tail = lax.slice_in_dim(cells, size - width, size, axis=dim)
    before = flat_permute(tail, axis, [(i, i + 1) for i in range(count - 1)])
    after = flat_permute(head, axis, [(i + 1, i) for i in range(count - 1)])
    return jnp.concatenate([before, cells, after], axis=dim)


def pinned(cells):
    return with_layout_constraint(cells, Layout(major_to_minor=tuple(range(cells.ndim))))


def with_ring(cells, width):
    rows_n = lax.axis_size("row")
    cols_n = lax.axis_size("col")
    tile_rows, tile_cols = cells.shape[0], cells.shape[1]
    down = [(i, i + 1) for i in range(rows_n - 1)]
    up = [(i + 1, i) for i in range(rows_n - 1)]
    right = [(i, i + 1) for i in range(cols_n - 1)]
    left = [(i + 1, i) for i in range(cols_n - 1)]
    top = flat_permute(cells[tile_rows - width:], "row", down)
    bottom = flat_permute(cells[:width], "row", up)
    west = lax.ppermute(cells[:, tile_cols - width:], "col", right)
    east = lax.ppermute(cells[:, :width], "col", left)
    rims = jnp.concatenate([top, bottom], axis=0)
    rim_west = lax.ppermute(rims[:, tile_cols - width:], "col", right)
    rim_east = lax.ppermute(rims[:, :width], "col", left)
    return jnp.concatenate(
        [
            jnp.concatenate([rim_west[:width], top, rim_east[:width]], axis=1),
            jnp.concatenate([west, cells, east], axis=1),
            jnp.concatenate([rim_west[width:], bottom, rim_east[width:]], axis=1),
        ],
        axis=0,
    )


def inside_mask(axis, tile, width):
    count = lax.axis_size(axis)
    start = lax.axis_index(axis) * tile - width
    index = start + jnp.arange(tile + 2 * width, dtype=jnp.int32)
    return (index >= 0) & (index < count * tile)


def sweep(field, source, keep):
    diff_col = field[:-1, 1:] - field[:-1, :-1]
    diff_row = field[1:, :-1] - field[:-1, :-1]
    energy_sum = jnp.sum(diff_col * diff_col + diff_row * diff_row, axis=-1, keepdims=True)
    weight = 1.0 / jnp.sqrt(1.0 + energy_sum / field.shape[-1])
    centre = field[1:-1, 1:-1]
    col_here = weight[1:, 1:] * (field[1:-1, 2:] - centre)
    col_left = weight[1:, :-1] * (centre - field[1:-1, :-2])
    row_here = weight[1:, 1:] * (field[2:, 1:-1] - centre)
    row_up = weight[:-1, 1:] * (centre - field[:-2, 1:-1])
    spread = col_here - col_left + row_here - row_up
    new = centre + tau_step * spread + tau_step * fidelity * (source - centre)
    return jnp.where(keep, new, 0.0)


def cholesky_qr(block):
    size = block.shape[1]
    inner = lax.dot_general(
        block, block, (((0,), (0,)), ((), ())),
        precision=lax.Precision.HIGHEST, preferred_element_type=jnp.float32,
    )
    sub = lax.broadcasted_iota(jnp.int32, (size, size), 0)
    lane = lax.broadcasted_iota(jnp.int32, (size, size), 1)
    upper = jnp.zeros((size, size), jnp.float32)
    inverse = jnp.zeros((size, size), jnp.float32)
    rest = inner
    for j in range(size):
        col = rest[:, j:j + 1]
        row = rest[j:j + 1, :]
        pivot = jnp.sqrt(rest[j:j + 1, j:j + 1])
        col = jnp.where(sub[:, :1] >= j, col / pivot, 0.0)
        row = jnp.where(lane[:1] >= j, row / pivot, 0.0)
        upper = upper + jnp.where(sub == j, row, 0.0)
        rest = rest - col * row
        coef = upper[:, j:j + 1]
        diag = upper[j:j + 1, j:j + 1]
        acc = jnp.sum(jnp.where(sub[:, :1] < j, coef, 0.0) * inverse, axis=0, keepdims=True)
        unit = jnp.where(lane[:1] == j, 1.0, 0.0)
        inverse = inverse + jnp.where(sub == j, (unit - acc) / diag, 0.0)
    return lax.dot_general(
        block, inverse, (((1,), (1,)), ((), ())),
        precision=lax.Precision.HIGHEST, preferred_element_type=jnp.float32,
    )


def subspace_kernel(gram_ref, basis_ref, out_ref):
    basis = basis_ref[...]
    for turn in range(SUBIT):
        product = jnp.dot(
            gram_ref[...], basis,
            precision=lax.Precision.HIGHEST, preferred_element_type=jnp.float32,
        )
        basis = cholesky_qr(cholesky_qr(product))
    out_ref[...] = basis


def subspace_step(gram_full, basis):
    return pl.pallas_call(
        subspace_kernel,
        out_shape=jax.ShapeDtypeStruct(basis.shape, jnp.float32),
        cost_estimate=pl.CostEstimate(
            flops=SUBIT * (2 * gram_full.shape[0] * gram_full.size + 8 * basis.size * basis.shape[1]),
            transcendentals=SUBIT * 2 * basis.shape[1],
            bytes_accessed=4 * (gram_full.size + 2 * basis.size),
        ),
    )(gram_full, basis)


def orthonormal(block):
    inner = jnp.dot(block.T, block, precision=lax.Precision.HIGHEST)
    lower = jnp.linalg.cholesky(inner)
    return lax.linalg.triangular_solve(lower, block, left_side=False, lower=True, transpose_a=True)


def shards(order, image, start_basis):
    band_count, tile_rows, tile_cols = image.shape
    width = SWEEPS
    cells = pinned(jnp.transpose(image, (1, 2, 0)))
    ext = with_ring(cells, width)
    row_in = inside_mask("row", tile_rows, width)
    col_in = inside_mask("col", tile_cols, width)
    field = ext
    for sweep_no in range(SWEEPS):
        left = width - sweep_no - 1
        lo = sweep_no + 1
        nr = tile_rows + 2 * left
        nc = tile_cols + 2 * left
        source = ext[lo:lo + nr, lo:lo + nc]
        keep = (row_in[lo:lo + nr, None] & col_in[None, lo:lo + nc])[:, :, None]
        field = pinned(sweep(field, source, keep))
    flat_cells = field.reshape(tile_rows * tile_cols, band_count)
    smoothed = jnp.transpose(field, (2, 0, 1))
    local_gram = lax.dot_general(
        flat_cells,
        flat_cells,
        (((0,), (0,)), ((), ())),
        precision=lax.Precision.HIGHEST,
        preferred_element_type=jnp.float32,
    )
    gram_full = paired_sum(local_gram, order)
    basis_now = start_basis
    basis_now = subspace_step(gram_full, basis_now)
    coeffs = jnp.dot(flat_cells, basis_now, precision=lax.Precision.HIGHEST)
    lowrank = lax.dot_general(
        basis_now,
        coeffs,
        (((1,), (1,)), ((), ())),
        precision=lax.Precision.HIGHEST,
    )
    return (smoothed, lowrank.reshape(band_count, tile_rows, tile_cols))


def solution(mesh):
    in_specs = (P(None, "row", "col"), P())
    out_specs = (P(None, "row", "col"), P(None, "row", "col"))
    body = functools.partial(shards, core_first(mesh))
    return jax.shard_map(body, mesh=mesh, in_specs=in_specs, out_specs=out_specs, check_vma=False)
```

```python
import functools

import jax
import jax.numpy as jnp
from jax import lax
from jax.sharding import PartitionSpec as P
from jax.experimental import pallas as pl
from jax.experimental.layout import Layout, with_layout_constraint
from jax.experimental.pallas import tpu as pltpu

SWEEPS = 4
SUBIT = 2


tau_step = 0.22
fidelity = 0.1


def butterfly_sum(value, axes, start=1):
    for axis in axes:
        count = lax.axis_size(axis)
        if count & (count - 1):
            value = lax.psum(value, axis)
            continue
        step = start if axis == axes[0] else 1
        while step < count:
            partner = lax.ppermute(value, axis, [(i, i ^ step) for i in range(count)])
            value = value + partner
            step *= 2
    return value


def paired_sum(value, axes):
    first = axes[0]
    count = lax.axis_size(first)
    half = value.shape[0] // 2
    if count < 2 or count & (count - 1) or value.shape[0] % 2:
        return butterfly_sum(value, axes)
    pairs = [(i, i ^ 1) for i in range(count)]
    low = lax.axis_index(first) % 2 == 0
    top, bottom = value[:half], value[half:]
    keep = jnp.where(low, top, bottom)
    give = jnp.where(low, bottom, top)
    part = keep + lax.ppermute(give, first, pairs)
    part = butterfly_sum(part, axes, start=2)
    other = lax.ppermute(part, first, pairs)
    return jnp.where(low, jnp.concatenate([part, other]), jnp.concatenate([other, part]))


def core_first(mesh):
    names = tuple(mesh.axis_names)
    devices = mesh.devices
    for pos, name in enumerate(names):
        if devices.shape[pos] < 2:
            continue
        at = [0] * devices.ndim
        one = devices[tuple(at)]
        at[pos] = 1
        two = devices[tuple(at)]
        coords = getattr(one, "coords", None)
        if coords is not None and tuple(coords) == tuple(getattr(two, "coords", ())):
            return (name,) + tuple(n for n in names if n != name)
    return names


def flat_permute(block, axis, pairs):
    pixels = block.size // block.shape[-1]
    if pixels % 64 or pixels <= block.shape[-1]:
        return lax.ppermute(block, axis, pairs)
    flat = block.reshape(pixels // 64, 64, block.shape[-1])
    return lax.ppermute(flat, axis, pairs).reshape(block.shape)


def with_halo(cells, axis, dim, width):
    count = lax.axis_size(axis)
    size = cells.shape[dim]
    head = lax.slice_in_dim(cells, 0, width, axis=dim)
    tail = lax.slice_in_dim(cells, size - width, size, axis=dim)
    before = flat_permute(tail, axis, [(i, i + 1) for i in range(count - 1)])
    after = flat_permute(head, axis, [(i + 1, i) for i in range(count - 1)])
    return jnp.concatenate([before, cells, after], axis=dim)


def pinned(cells):
    return with_layout_constraint(cells, Layout(major_to_minor=tuple(range(cells.ndim))))


def with_ring(cells, width):
    rows_n = lax.axis_size("row")
    cols_n = lax.axis_size("col")
    tile_rows, tile_cols = cells.shape[0], cells.shape[1]
    down = [(i, i + 1) for i in range(rows_n - 1)]
    up = [(i + 1, i) for i in range(rows_n - 1)]
    right = [(i, i + 1) for i in range(cols_n - 1)]
    left = [(i + 1, i) for i in range(cols_n - 1)]
    top = flat_permute(cells[tile_rows - width:], "row", down)
    bottom = flat_permute(cells[:width], "row", up)
    west = lax.ppermute(cells[:, tile_cols - width:], "col", right)
    east = lax.ppermute(cells[:, :width], "col", left)
    rims = jnp.concatenate([top, bottom], axis=0)
    rim_west = lax.ppermute(rims[:, tile_cols - width:], "col", right)
    rim_east = lax.ppermute(rims[:, :width], "col", left)
    return jnp.concatenate(
        [
            jnp.concatenate([rim_west[:width], top, rim_east[:width]], axis=1),
            jnp.concatenate([west, cells, east], axis=1),
            jnp.concatenate([rim_west[width:], bottom, rim_east[width:]], axis=1),
        ],
        axis=0,
    )


def inside_mask(axis, tile, width):
    count = lax.axis_size(axis)
    start = lax.axis_index(axis) * tile - width
    index = start + jnp.arange(tile + 2 * width, dtype=jnp.int32)
    return (index >= 0) & (index < count * tile)


def sweep(field, source, keep):
    diff_col = field[:-1, 1:] - field[:-1, :-1]
    diff_row = field[1:, :-1] - field[:-1, :-1]
    energy_sum = jnp.sum(diff_col * diff_col + diff_row * diff_row, axis=-1, keepdims=True)
    weight = 1.0 / jnp.sqrt(1.0 + energy_sum / field.shape[-1])
    centre = field[1:-1, 1:-1]
    col_here = weight[1:, 1:] * (field[1:-1, 2:] - centre)
    col_left = weight[1:, :-1] * (centre - field[1:-1, :-2])
    row_here = weight[1:, 1:] * (field[2:, 1:-1] - centre)
    row_up = weight[:-1, 1:] * (centre - field[:-2, 1:-1])
    spread = col_here - col_left + row_here - row_up
    new = centre + tau_step * spread + tau_step * fidelity * (source - centre)
    return jnp.where(keep, new, 0.0)


def cholesky_qr(block):
    size = block.shape[1]
    inner = lax.dot_general(
        block, block, (((0,), (0,)), ((), ())),
        precision=lax.Precision.HIGHEST, preferred_element_type=jnp.float32,
    )
    sub = lax.broadcasted_iota(jnp.int32, (size, size), 0)
    lane = lax.broadcasted_iota(jnp.int32, (size, size), 1)
    upper = jnp.zeros((size, size), jnp.float32)
    inverse = jnp.zeros((size, size), jnp.float32)
    rest = inner
    for j in range(size):
        col = rest[:, j:j + 1]
        row = rest[j:j + 1, :]
        pivot = jnp.sqrt(rest[j:j + 1, j:j + 1])
        col = jnp.where(sub[:, :1] >= j, col / pivot, 0.0)
        row = jnp.where(lane[:1] >= j, row / pivot, 0.0)
        upper = upper + jnp.where(sub == j, row, 0.0)
        rest = rest - col * row
        coef = upper[:, j:j + 1]
        diag = upper[j:j + 1, j:j + 1]
        acc = jnp.sum(jnp.where(sub[:, :1] < j, coef, 0.0) * inverse, axis=0, keepdims=True)
        unit = jnp.where(lane[:1] == j, 1.0, 0.0)
        inverse = inverse + jnp.where(sub == j, (unit - acc) / diag, 0.0)
    return lax.dot_general(
        block, inverse, (((1,), (1,)), ((), ())),
        precision=lax.Precision.HIGHEST, preferred_element_type=jnp.float32,
    )


def subspace_kernel(gram_ref, basis_ref, out_ref):
    basis = basis_ref[...]
    for turn in range(SUBIT):
        product = jnp.dot(
            gram_ref[...], basis,
            precision=lax.Precision.HIGHEST, preferred_element_type=jnp.float32,
        )
        basis = cholesky_qr(cholesky_qr(product))
    out_ref[...] = basis


def subspace_step(gram_full, basis):
    return pl.pallas_call(
        subspace_kernel,
        out_shape=jax.ShapeDtypeStruct(basis.shape, jnp.float32),
        cost_estimate=pl.CostEstimate(
            flops=SUBIT * (2 * gram_full.shape[0] * gram_full.size + 8 * basis.size * basis.shape[1]),
            transcendentals=SUBIT * 2 * basis.shape[1],
            bytes_accessed=4 * (gram_full.size + 2 * basis.size),
        ),
    )(gram_full, basis)


def orthonormal(block):
    inner = jnp.dot(block.T, block, precision=lax.Precision.HIGHEST)
    lower = jnp.linalg.cholesky(inner)
    return lax.linalg.triangular_solve(lower, block, left_side=False, lower=True, transpose_a=True)


def shards(order, image, start_basis):
    band_count, tile_rows, tile_cols = image.shape
    width = SWEEPS
    cells = pinned(jnp.transpose(image, (1, 2, 0)))
    ext = with_ring(cells, width)
    row_in = inside_mask("row", tile_rows, width)
    col_in = inside_mask("col", tile_cols, width)
    field = ext
    for sweep_no in range(SWEEPS):
        left = width - sweep_no - 1
        lo = sweep_no + 1
        nr = tile_rows + 2 * left
        nc = tile_cols + 2 * left
        source = ext[lo:lo + nr, lo:lo + nc]
        keep = (row_in[lo:lo + nr, None] & col_in[None, lo:lo + nc])[:, :, None]
        field = pinned(sweep(field, source, keep))
    flat_cells = field.reshape(tile_rows * tile_cols, band_count)
    smoothed = jnp.transpose(field, (2, 0, 1))
    local_gram = lax.dot_general(
        flat_cells,
        flat_cells,
        (((0,), (0,)), ((), ())),
        precision=lax.Precision.HIGHEST,
        preferred_element_type=jnp.float32,
    )
    gram_full = paired_sum(local_gram, order)
    basis_now = start_basis
    basis_now = subspace_step(gram_full, basis_now)
    coeffs = lax.dot_general(
        basis_now,
        smoothed,
        (((0,), (0,)), ((), ())),
        precision=lax.Precision.HIGHEST,
        preferred_element_type=jnp.float32,
    )
    lowrank = lax.dot_general(
        basis_now,
        coeffs,
        (((1,), (0,)), ((), ())),
        precision=lax.Precision.HIGHEST,
        preferred_element_type=jnp.float32,
    )
    return (smoothed, lowrank)


def solution(mesh):
    in_specs = (P(None, "row", "col"), P())
    out_specs = (P(None, "row", "col"), P(None, "row", "col"))
    body = functools.partial(shards, core_first(mesh))
    return jax.shard_map(body, mesh=mesh, in_specs=in_specs, out_specs=out_specs, check_vma=False)
```

```python
import functools

import jax
import jax.numpy as jnp
from jax import lax
from jax.sharding import PartitionSpec as P
from jax.experimental import pallas as pl
from jax.experimental.layout import Layout, with_layout_constraint
from jax.experimental.pallas import tpu as pltpu

SWEEPS = 4
SUBIT = 2


tau_step = 0.22
fidelity = 0.1


def butterfly_sum(value, axes, start=1):
    for axis in axes:
        count = lax.axis_size(axis)
        if count & (count - 1):
            value = lax.psum(value, axis)
            continue
        step = start if axis == axes[0] else 1
        while step < count:
            partner = lax.ppermute(value, axis, [(i, i ^ step) for i in range(count)])
            value = value + partner
            step *= 2
    return value


def paired_sum(value, axes):
    first = axes[0]
    count = lax.axis_size(first)
    half = value.shape[0] // 2
    if count < 2 or count & (count - 1) or value.shape[0] % 2:
        return butterfly_sum(value, axes)
    pairs = [(i, i ^ 1) for i in range(count)]
    low = lax.axis_index(first) % 2 == 0
    top, bottom = value[:half], value[half:]
    keep = jnp.where(low, top, bottom)
    give = jnp.where(low, bottom, top)
    part = keep + lax.ppermute(give, first, pairs)
    part = butterfly_sum(part, axes, start=2)
    other = lax.ppermute(part, first, pairs)
    return jnp.where(low, jnp.concatenate([part, other]), jnp.concatenate([other, part]))


def core_first(mesh):
    names = tuple(mesh.axis_names)
    devices = mesh.devices
    for pos, name in enumerate(names):
        if devices.shape[pos] < 2:
            continue
        at = [0] * devices.ndim
        one = devices[tuple(at)]
        at[pos] = 1
        two = devices[tuple(at)]
        coords = getattr(one, "coords", None)
        if coords is not None and tuple(coords) == tuple(getattr(two, "coords", ())):
            return (name,) + tuple(n for n in names if n != name)
    return names


def flat_permute(block, axis, pairs):
    pixels = block.size // block.shape[-1]
    if pixels % 64 or pixels <= block.shape[-1]:
        return lax.ppermute(block, axis, pairs)
    flat = block.reshape(pixels // 64, 64, block.shape[-1])
    return lax.ppermute(flat, axis, pairs).reshape(block.shape)


def with_halo(cells, axis, dim, width):
    count = lax.axis_size(axis)
    size = cells.shape[dim]
    head = lax.slice_in_dim(cells, 0, width, axis=dim)
    tail = lax.slice_in_dim(cells, size - width, size, axis=dim)
    before = flat_permute(tail, axis, [(i, i + 1) for i in range(count - 1)])
    after = flat_permute(head, axis, [(i + 1, i) for i in range(count - 1)])
    return jnp.concatenate([before, cells, after], axis=dim)


def pinned(cells):
    return with_layout_constraint(cells, Layout(major_to_minor=tuple(range(cells.ndim))))


def with_ring(cells, width):
    rows_n = lax.axis_size("row")
    cols_n = lax.axis_size("col")
    tile_rows, tile_cols = cells.shape[0], cells.shape[1]
    down = [(i, i + 1) for i in range(rows_n - 1)]
    up = [(i + 1, i) for i in range(rows_n - 1)]
    right = [(i, i + 1) for i in range(cols_n - 1)]
    left = [(i + 1, i) for i in range(cols_n - 1)]
    top = flat_permute(cells[tile_rows - width:], "row", down)
    bottom = flat_permute(cells[:width], "row", up)
    west = lax.ppermute(cells[:, tile_cols - width:], "col", right)
    east = lax.ppermute(cells[:, :width], "col", left)
    rims = jnp.concatenate([top, bottom], axis=0)
    rim_west = lax.ppermute(rims[:, tile_cols - width:], "col", right)
    rim_east = lax.ppermute(rims[:, :width], "col", left)
    return jnp.concatenate(
        [
            jnp.concatenate([rim_west[:width], top, rim_east[:width]], axis=1),
            jnp.concatenate([west, cells, east], axis=1),
            jnp.concatenate([rim_west[width:], bottom, rim_east[width:]], axis=1),
        ],
        axis=0,
    )


def inside_mask(axis, tile, width):
    count = lax.axis_size(axis)
    start = lax.axis_index(axis) * tile - width
    index = start + jnp.arange(tile + 2 * width, dtype=jnp.int32)
    return (index >= 0) & (index < count * tile)


def sweep(field, source, keep):
    diff_col = field[:-1, 1:] - field[:-1, :-1]
    diff_row = field[1:, :-1] - field[:-1, :-1]
    energy_sum = jnp.sum(diff_col * diff_col + diff_row * diff_row, axis=-1, keepdims=True)
    weight = 1.0 / jnp.sqrt(1.0 + energy_sum / field.shape[-1])
    centre = field[1:-1, 1:-1]
    col_here = weight[1:, 1:] * (field[1:-1, 2:] - centre)
    col_left = weight[1:, :-1] * (centre - field[1:-1, :-2])
    row_here = weight[1:, 1:] * (field[2:, 1:-1] - centre)
    row_up = weight[:-1, 1:] * (centre - field[:-2, 1:-1])
    spread = col_here - col_left + row_here - row_up
    new = centre + tau_step * spread + tau_step * fidelity * (source - centre)
    return jnp.where(keep, new, 0.0)


def cholesky_qr(block):
    size = block.shape[1]
    inner = lax.dot_general(
        block, block, (((0,), (0,)), ((), ())),
        precision=lax.Precision.HIGHEST, preferred_element_type=jnp.float32,
    )
    sub = lax.broadcasted_iota(jnp.int32, (size, size), 0)
    lane = lax.broadcasted_iota(jnp.int32, (size, size), 1)
    upper = jnp.zeros((size, size), jnp.float32)
    inverse = jnp.zeros((size, size), jnp.float32)
    rest = inner
    for j in range(size):
        col = rest[:, j:j + 1]
        row = rest[j:j + 1, :]
        pivot = jnp.sqrt(rest[j:j + 1, j:j + 1])
        col = jnp.where(sub[:, :1] >= j, col / pivot, 0.0)
        row = jnp.where(lane[:1] >= j, row / pivot, 0.0)
        upper = upper + jnp.where(sub == j, row, 0.0)
        rest = rest - col * row
        coef = upper[:, j:j + 1]
        diag = upper[j:j + 1, j:j + 1]
        acc = jnp.sum(jnp.where(sub[:, :1] < j, coef, 0.0) * inverse, axis=0, keepdims=True)
        unit = jnp.where(lane[:1] == j, 1.0, 0.0)
        inverse = inverse + jnp.where(sub == j, (unit - acc) / diag, 0.0)
    return lax.dot_general(
        block, inverse, (((1,), (1,)), ((), ())),
        precision=lax.Precision.HIGHEST, preferred_element_type=jnp.float32,
    )


def subspace_kernel(gram_ref, basis_ref, out_ref):
    basis = basis_ref[...]
    for turn in range(SUBIT):
        product = jnp.dot(
            gram_ref[...], basis,
            precision=lax.Precision.HIGHEST, preferred_element_type=jnp.float32,
        )
        basis = cholesky_qr(cholesky_qr(product))
    out_ref[...] = basis


def subspace_step(gram_full, basis):
    return pl.pallas_call(
        subspace_kernel,
        out_shape=jax.ShapeDtypeStruct(basis.shape, jnp.float32),
        cost_estimate=pl.CostEstimate(
            flops=SUBIT * (2 * gram_full.shape[0] * gram_full.size + 8 * basis.size * basis.shape[1]),
            transcendentals=SUBIT * 2 * basis.shape[1],
            bytes_accessed=4 * (gram_full.size + 2 * basis.size),
        ),
    )(gram_full, basis)


def orthonormal(block):
    inner = jnp.dot(block.T, block, precision=lax.Precision.HIGHEST)
    lower = jnp.linalg.cholesky(inner)
    return lax.linalg.triangular_solve(lower, block, left_side=False, lower=True, transpose_a=True)


def shards(order, image, start_basis):
    band_count, tile_rows, tile_cols = image.shape
    width = SWEEPS
    cells = pinned(jnp.transpose(image, (1, 2, 0)))
    ext = with_ring(cells, width)
    row_in = inside_mask("row", tile_rows, width)
    col_in = inside_mask("col", tile_cols, width)
    field = ext
    for sweep_no in range(SWEEPS):
        left = width - sweep_no - 1
        lo = sweep_no + 1
        nr = tile_rows + 2 * left
        nc = tile_cols + 2 * left
        source = ext[lo:lo + nr, lo:lo + nc]
        keep = (row_in[lo:lo + nr, None] & col_in[None, lo:lo + nc])[:, :, None]
        field = pinned(sweep(field, source, keep))
    flat_cells = field.reshape(tile_rows * tile_cols, band_count)
    smoothed = jnp.transpose(field, (2, 0, 1))
    local_gram = lax.dot_general(
        flat_cells,
        flat_cells,
        (((0,), (0,)), ((), ())),
        precision=lax.Precision.HIGH,
        preferred_element_type=jnp.float32,
    )
    gram_full = paired_sum(local_gram, order)
    basis_now = start_basis
    basis_now = subspace_step(gram_full, basis_now)
    coeffs = jnp.dot(flat_cells, basis_now, precision=lax.Precision.HIGH)
    lowrank = lax.dot_general(
        basis_now,
        coeffs,
        (((1,), (1,)), ((), ())),
        precision=lax.Precision.HIGH,
    )
    return (smoothed, lowrank.reshape(band_count, tile_rows, tile_cols))


def solution(mesh):
    in_specs = (P(None, "row", "col"), P())
    out_specs = (P(None, "row", "col"), P(None, "row", "col"))
    body = functools.partial(shards, core_first(mesh))
    return jax.shard_map(body, mesh=mesh, in_specs=in_specs, out_specs=out_specs, check_vma=False)
```

```python
import functools

import jax
import jax.numpy as jnp
from jax import lax
from jax.sharding import PartitionSpec as P
from jax.experimental import pallas as pl
from jax.experimental.layout import Layout, with_layout_constraint
from jax.experimental.pallas import tpu as pltpu

SWEEPS = 4
SUBIT = 2


tau_step = 0.22
fidelity = 0.1


def butterfly_sum(value, axes, start=1):
    for axis in axes:
        count = lax.axis_size(axis)
        if count & (count - 1):
            value = lax.psum(value, axis)
            continue
        step = start if axis == axes[0] else 1
        while step < count:
            partner = lax.ppermute(value, axis, [(i, i ^ step) for i in range(count)])
            value = value + partner
            step *= 2
    return value


def paired_sum(value, axes):
    first = axes[0]
    count = lax.axis_size(first)
    half = value.shape[0] // 2
    if count < 2 or count & (count - 1) or value.shape[0] % 2:
        return butterfly_sum(value, axes)
    pairs = [(i, i ^ 1) for i in range(count)]
    low = lax.axis_index(first) % 2 == 0
    top, bottom = value[:half], value[half:]
    keep = jnp.where(low, top, bottom)
    give = jnp.where(low, bottom, top)
    part = keep + lax.ppermute(give, first, pairs)
    part = butterfly_sum(part, axes, start=2)
    other = lax.ppermute(part, first, pairs)
    return jnp.where(low, jnp.concatenate([part, other]), jnp.concatenate([other, part]))


def core_first(mesh):
    names = tuple(mesh.axis_names)
    devices = mesh.devices
    for pos, name in enumerate(names):
        if devices.shape[pos] < 2:
            continue
        at = [0] * devices.ndim
        one = devices[tuple(at)]
        at[pos] = 1
        two = devices[tuple(at)]
        coords = getattr(one, "coords", None)
        if coords is not None and tuple(coords) == tuple(getattr(two, "coords", ())):
            return (name,) + tuple(n for n in names if n != name)
    return names


def flat_permute(block, axis, pairs):
    pixels = block.size // block.shape[-1]
    if pixels % 64 or pixels <= block.shape[-1]:
        return lax.ppermute(block, axis, pairs)
    flat = block.reshape(pixels // 64, 64, block.shape[-1])
    return lax.ppermute(flat, axis, pairs).reshape(block.shape)


def with_halo(cells, axis, dim, width):
    count = lax.axis_size(axis)
    size = cells.shape[dim]
    head = lax.slice_in_dim(cells, 0, width, axis=dim)
    tail = lax.slice_in_dim(cells, size - width, size, axis=dim)
    before = flat_permute(tail, axis, [(i, i + 1) for i in range(count - 1)])
    after = flat_permute(head, axis, [(i + 1, i) for i in range(count - 1)])
    return jnp.concatenate([before, cells, after], axis=dim)


def pinned(cells):
    return with_layout_constraint(cells, Layout(major_to_minor=tuple(range(cells.ndim))))


def with_ring(cells, width):
    rows_n = lax.axis_size("row")
    cols_n = lax.axis_size("col")
    tile_rows, tile_cols = cells.shape[0], cells.shape[1]
    down = [(i, i + 1) for i in range(rows_n - 1)]
    up = [(i + 1, i) for i in range(rows_n - 1)]
    right = [(i, i + 1) for i in range(cols_n - 1)]
    left = [(i + 1, i) for i in range(cols_n - 1)]
    top = flat_permute(cells[tile_rows - width:], "row", down)
    bottom = flat_permute(cells[:width], "row", up)
    west = lax.ppermute(cells[:, tile_cols - width:], "col", right)
    east = lax.ppermute(cells[:, :width], "col", left)
    rims = jnp.concatenate([top, bottom], axis=0)
    rim_west = lax.ppermute(rims[:, tile_cols - width:], "col", right)
    rim_east = lax.ppermute(rims[:, :width], "col", left)
    return jnp.concatenate(
        [
            jnp.concatenate([rim_west[:width], top, rim_east[:width]], axis=1),
            jnp.concatenate([west, cells, east], axis=1),
            jnp.concatenate([rim_west[width:], bottom, rim_east[width:]], axis=1),
        ],
        axis=0,
    )


def inside_mask(axis, tile, width):
    count = lax.axis_size(axis)
    start = lax.axis_index(axis) * tile - width
    index = start + jnp.arange(tile + 2 * width, dtype=jnp.int32)
    return (index >= 0) & (index < count * tile)


def sweep(field, source, keep):
    diff_col = field[:-1, 1:] - field[:-1, :-1]
    diff_row = field[1:, :-1] - field[:-1, :-1]
    energy_sum = jnp.sum(diff_col * diff_col + diff_row * diff_row, axis=-1, keepdims=True)
    weight = 1.0 / jnp.sqrt(1.0 + energy_sum / field.shape[-1])
    centre = field[1:-1, 1:-1]
    col_here = weight[1:, 1:] * (field[1:-1, 2:] - centre)
    col_left = weight[1:, :-1] * (centre - field[1:-1, :-2])
    row_here = weight[1:, 1:] * (field[2:, 1:-1] - centre)
    row_up = weight[:-1, 1:] * (centre - field[:-2, 1:-1])
    spread = col_here - col_left + row_here - row_up
    new = centre + tau_step * spread + tau_step * fidelity * (source - centre)
    return jnp.where(keep, new, 0.0)


def cholesky_qr(block):
    size = block.shape[1]
    inner = lax.dot_general(
        block, block, (((0,), (0,)), ((), ())),
        precision=lax.Precision.HIGHEST, preferred_element_type=jnp.float32,
    )
    sub = lax.broadcasted_iota(jnp.int32, (size, size), 0)
    lane = lax.broadcasted_iota(jnp.int32, (size, size), 1)
    upper = jnp.zeros((size, size), jnp.float32)
    inverse = jnp.zeros((size, size), jnp.float32)
    rest = inner
    for j in range(size):
        col = rest[:, j:j + 1]
        row = rest[j:j + 1, :]
        pivot = jnp.sqrt(rest[j:j + 1, j:j + 1])
        col = jnp.where(sub[:, :1] >= j, col / pivot, 0.0)
        row = jnp.where(lane[:1] >= j, row / pivot, 0.0)
        upper = upper + jnp.where(sub == j, row, 0.0)
        rest = rest - col * row
        coef = upper[:, j:j + 1]
        diag = upper[j:j + 1, j:j + 1]
        acc = jnp.sum(jnp.where(sub[:, :1] < j, coef, 0.0) * inverse, axis=0, keepdims=True)
        unit = jnp.where(lane[:1] == j, 1.0, 0.0)
        inverse = inverse + jnp.where(sub == j, (unit - acc) / diag, 0.0)
    return lax.dot_general(
        block, inverse, (((1,), (1,)), ((), ())),
        precision=lax.Precision.HIGHEST, preferred_element_type=jnp.float32,
    )


def subspace_kernel(gram_ref, basis_ref, out_ref):
    basis = basis_ref[...]
    for turn in range(SUBIT):
        product = jnp.dot(
            gram_ref[...], basis,
            precision=lax.Precision.HIGHEST, preferred_element_type=jnp.float32,
        )
        basis = cholesky_qr(cholesky_qr(product))
    out_ref[...] = basis


def subspace_step(gram_full, basis):
    return pl.pallas_call(
        subspace_kernel,
        out_shape=jax.ShapeDtypeStruct(basis.shape, jnp.float32),
        cost_estimate=pl.CostEstimate(
            flops=SUBIT * (2 * gram_full.shape[0] * gram_full.size + 8 * basis.size * basis.shape[1]),
            transcendentals=SUBIT * 2 * basis.shape[1],
            bytes_accessed=4 * (gram_full.size + 2 * basis.size),
        ),
    )(gram_full, basis)


def orthonormal(block):
    inner = jnp.dot(block.T, block, precision=lax.Precision.HIGHEST)
    lower = jnp.linalg.cholesky(inner)
    return lax.linalg.triangular_solve(lower, block, left_side=False, lower=True, transpose_a=True)


def shards(order, image, start_basis):
    band_count, tile_rows, tile_cols = image.shape
    width = SWEEPS
    cells = pinned(jnp.transpose(image, (1, 2, 0)))
    ext = with_ring(cells, width)
    row_in = inside_mask("row", tile_rows, width)
    col_in = inside_mask("col", tile_cols, width)
    field = ext
    for sweep_no in range(SWEEPS):
        left = width - sweep_no - 1
        lo = sweep_no + 1
        nr = tile_rows + 2 * left
        nc = tile_cols + 2 * left
        source = ext[lo:lo + nr, lo:lo + nc]
        keep = (row_in[lo:lo + nr, None] & col_in[None, lo:lo + nc])[:, :, None]
        field = pinned(sweep(field, source, keep))
    flat_cells = field.reshape(tile_rows * tile_cols, band_count)
    smoothed = jnp.transpose(field, (2, 0, 1))
    local_gram = lax.dot_general(
        flat_cells,
        flat_cells,
        (((0,), (0,)), ((), ())),
        precision=lax.Precision.HIGHEST,
        preferred_element_type=jnp.float32,
    )
    gram_full = paired_sum(local_gram, order)
    basis_now = start_basis
    basis_now = subspace_step(gram_full, basis_now)
    coeffs = jnp.dot(flat_cells, basis_now, precision=lax.Precision.HIGH)
    lowrank = lax.dot_general(
        basis_now,
        coeffs,
        (((1,), (1,)), ((), ())),
        precision=lax.Precision.HIGH,
    )
    return (smoothed, lowrank.reshape(band_count, tile_rows, tile_cols))


def solution(mesh):
    in_specs = (P(None, "row", "col"), P())
    out_specs = (P(None, "row", "col"), P(None, "row", "col"))
    body = functools.partial(shards, core_first(mesh))
    return jax.shard_map(body, mesh=mesh, in_specs=in_specs, out_specs=out_specs, check_vma=False)
```

```python
import functools

import jax
import jax.numpy as jnp
from jax import lax
from jax.sharding import PartitionSpec as P
from jax.experimental import pallas as pl
from jax.experimental.layout import Layout, with_layout_constraint
from jax.experimental.pallas import tpu as pltpu

SWEEPS = 4
SUBIT = 2


tau_step = 0.22
fidelity = 0.1


def butterfly_sum(value, axes, start=1):
    for axis in axes:
        count = lax.axis_size(axis)
        if count & (count - 1):
            value = lax.psum(value, axis)
            continue
        step = start if axis == axes[0] else 1
        while step < count:
            partner = lax.ppermute(value, axis, [(i, i ^ step) for i in range(count)])
            value = value + partner
            step *= 2
    return value


def paired_sum(value, axes):
    first = axes[0]
    count = lax.axis_size(first)
    half = value.shape[0] // 2
    if count < 2 or count & (count - 1) or value.shape[0] % 2:
        return butterfly_sum(value, axes)
    pairs = [(i, i ^ 1) for i in range(count)]
    low = lax.axis_index(first) % 2 == 0
    top, bottom = value[:half], value[half:]
    keep = jnp.where(low, top, bottom)
    give = jnp.where(low, bottom, top)
    part = keep + lax.ppermute(give, first, pairs)
    part = butterfly_sum(part, axes, start=2)
    other = lax.ppermute(part, first, pairs)
    return jnp.where(low, jnp.concatenate([part, other]), jnp.concatenate([other, part]))


def core_first(mesh):
    names = tuple(mesh.axis_names)
    devices = mesh.devices
    for pos, name in enumerate(names):
        if devices.shape[pos] < 2:
            continue
        at = [0] * devices.ndim
        one = devices[tuple(at)]
        at[pos] = 1
        two = devices[tuple(at)]
        coords = getattr(one, "coords", None)
        if coords is not None and tuple(coords) == tuple(getattr(two, "coords", ())):
            return (name,) + tuple(n for n in names if n != name)
    return names


def flat_permute(block, axis, pairs):
    pixels = block.size // block.shape[-1]
    if pixels % 64 or pixels <= block.shape[-1]:
        return lax.ppermute(block, axis, pairs)
    flat = block.reshape(pixels // 64, 64, block.shape[-1])
    return lax.ppermute(flat, axis, pairs).reshape(block.shape)


def with_halo(cells, axis, dim, width):
    count = lax.axis_size(axis)
    size = cells.shape[dim]
    head = lax.slice_in_dim(cells, 0, width, axis=dim)
    tail = lax.slice_in_dim(cells, size - width, size, axis=dim)
    before = flat_permute(tail, axis, [(i, i + 1) for i in range(count - 1)])
    after = flat_permute(head, axis, [(i + 1, i) for i in range(count - 1)])
    return jnp.concatenate([before, cells, after], axis=dim)


def pinned(cells):
    return with_layout_constraint(cells, Layout(major_to_minor=tuple(range(cells.ndim))))


def with_ring(cells, width):
    rows_n = lax.axis_size("row")
    cols_n = lax.axis_size("col")
    tile_rows, tile_cols = cells.shape[0], cells.shape[1]
    down = [(i, i + 1) for i in range(rows_n - 1)]
    up = [(i + 1, i) for i in range(rows_n - 1)]
    right = [(i, i + 1) for i in range(cols_n - 1)]
    left = [(i + 1, i) for i in range(cols_n - 1)]
    top = flat_permute(cells[tile_rows - width:], "row", down)
    bottom = flat_permute(cells[:width], "row", up)
    west = lax.ppermute(cells[:, tile_cols - width:], "col", right)
    east = lax.ppermute(cells[:, :width], "col", left)
    rims = jnp.concatenate([top, bottom], axis=0)
    rim_west = lax.ppermute(rims[:, tile_cols - width:], "col", right)
    rim_east = lax.ppermute(rims[:, :width], "col", left)
    return jnp.concatenate(
        [
            jnp.concatenate([rim_west[:width], top, rim_east[:width]], axis=1),
            jnp.concatenate([west, cells, east], axis=1),
            jnp.concatenate([rim_west[width:], bottom, rim_east[width:]], axis=1),
        ],
        axis=0,
    )


def inside_mask(axis, tile, width):
    count = lax.axis_size(axis)
    start = lax.axis_index(axis) * tile - width
    index = start + jnp.arange(tile + 2 * width, dtype=jnp.int32)
    return (index >= 0) & (index < count * tile)


def sweep(field, source, keep):
    diff_col = field[:-1, 1:] - field[:-1, :-1]
    diff_row = field[1:, :-1] - field[:-1, :-1]
    energy_sum = jnp.sum(diff_col * diff_col + diff_row * diff_row, axis=-1, keepdims=True)
    weight = 1.0 / jnp.sqrt(1.0 + energy_sum / field.shape[-1])
    centre = field[1:-1, 1:-1]
    col_here = weight[1:, 1:] * (field[1:-1, 2:] - centre)
    col_left = weight[1:, :-1] * (centre - field[1:-1, :-2])
    row_here = weight[1:, 1:] * (field[2:, 1:-1] - centre)
    row_up = weight[:-1, 1:] * (centre - field[:-2, 1:-1])
    spread = col_here - col_left + row_here - row_up
    new = centre + tau_step * spread + tau_step * fidelity * (source - centre)
    return jnp.where(keep, new, 0.0)


def cholesky_qr(block):
    size = block.shape[1]
    inner = lax.dot_general(
        block, block, (((0,), (0,)), ((), ())),
        precision=lax.Precision.HIGHEST, preferred_element_type=jnp.float32,
    )
    sub = lax.broadcasted_iota(jnp.int32, (size, size), 0)
    lane = lax.broadcasted_iota(jnp.int32, (size, size), 1)
    upper = jnp.zeros((size, size), jnp.float32)
    inverse = jnp.zeros((size, size), jnp.float32)
    rest = inner
    for j in range(size):
        col = rest[:, j:j + 1]
        row = rest[j:j + 1, :]
        pivot = jnp.sqrt(rest[j:j + 1, j:j + 1])
        col = jnp.where(sub[:, :1] >= j, col / pivot, 0.0)
        row = jnp.where(lane[:1] >= j, row / pivot, 0.0)
        upper = upper + jnp.where(sub == j, row, 0.0)
        rest = rest - col * row
        coef = upper[:, j:j + 1]
        diag = upper[j:j + 1, j:j + 1]
        acc = jnp.sum(jnp.where(sub[:, :1] < j, coef, 0.0) * inverse, axis=0, keepdims=True)
        unit = jnp.where(lane[:1] == j, 1.0, 0.0)
        inverse = inverse + jnp.where(sub == j, (unit - acc) / diag, 0.0)
    return lax.dot_general(
        block, inverse, (((1,), (1,)), ((), ())),
        precision=lax.Precision.HIGHEST, preferred_element_type=jnp.float32,
    )


def subspace_kernel(gram_ref, basis_ref, out_ref):
    basis = basis_ref[...]
    for turn in range(SUBIT):
        product = jnp.dot(
            gram_ref[...], basis,
            precision=lax.Precision.HIGHEST, preferred_element_type=jnp.float32,
        )
        basis = cholesky_qr(cholesky_qr(product))
    out_ref[...] = basis


def subspace_step(gram_full, basis):
    return pl.pallas_call(
        subspace_kernel,
        out_shape=jax.ShapeDtypeStruct(basis.shape, jnp.float32),
        cost_estimate=pl.CostEstimate(
            flops=SUBIT * (2 * gram_full.shape[0] * gram_full.size + 8 * basis.size * basis.shape[1]),
            transcendentals=SUBIT * 2 * basis.shape[1],
            bytes_accessed=4 * (gram_full.size + 2 * basis.size),
        ),
    )(gram_full, basis)


def orthonormal(block):
    inner = jnp.dot(block.T, block, precision=lax.Precision.HIGHEST)
    lower = jnp.linalg.cholesky(inner)
    return lax.linalg.triangular_solve(lower, block, left_side=False, lower=True, transpose_a=True)


def shards(order, image, start_basis):
    band_count, tile_rows, tile_cols = image.shape
    width = SWEEPS
    cells = pinned(jnp.transpose(image, (1, 2, 0)))
    ext = with_ring(cells, width)
    row_in = inside_mask("row", tile_rows, width)
    col_in = inside_mask("col", tile_cols, width)
    field = ext
    for sweep_no in range(SWEEPS):
        left = width - sweep_no - 1
        lo = sweep_no + 1
        nr = tile_rows + 2 * left
        nc = tile_cols + 2 * left
        source = ext[lo:lo + nr, lo:lo + nc]
        keep = (row_in[lo:lo + nr, None] & col_in[None, lo:lo + nc])[:, :, None]
        field = pinned(sweep(field, source, keep))
    flat_cells = field.reshape(tile_rows * tile_cols, band_count)
    smoothed = jnp.transpose(field, (2, 0, 1))
    local_gram = lax.dot_general(
        flat_cells,
        flat_cells,
        (((0,), (0,)), ((), ())),
        precision=lax.Precision.HIGHEST,
        preferred_element_type=jnp.float32,
    )
    gram_full = paired_sum(local_gram, order)
    basis_now = start_basis
    basis_now = subspace_step(gram_full, basis_now)
    coeffs = lax.dot_general(
        basis_now,
        flat_cells,
        (((0,), (1,)), ((), ())),
        precision=lax.Precision.HIGH,
        preferred_element_type=jnp.float32,
    )
    lowrank = jnp.dot(basis_now, coeffs, precision=lax.Precision.HIGH)
    return (smoothed, lowrank.reshape(band_count, tile_rows, tile_cols))


def solution(mesh):
    in_specs = (P(None, "row", "col"), P())
    out_specs = (P(None, "row", "col"), P(None, "row", "col"))
    body = functools.partial(shards, core_first(mesh))
    return jax.shard_map(body, mesh=mesh, in_specs=in_specs, out_specs=out_specs, check_vma=False)
```

```python
import functools

import jax
import jax.numpy as jnp
from jax import lax
from jax.sharding import PartitionSpec as P
from jax.experimental import pallas as pl
from jax.experimental.layout import Layout, with_layout_constraint
from jax.experimental.pallas import tpu as pltpu

SWEEPS = 4
SUBIT = 2


tau_step = 0.22
fidelity = 0.1


def butterfly_sum(value, axes, start=1):
    for axis in axes:
        count = lax.axis_size(axis)
        if count & (count - 1):
            value = lax.psum(value, axis)
            continue
        step = start if axis == axes[0] else 1
        while step < count:
            partner = lax.ppermute(value, axis, [(i, i ^ step) for i in range(count)])
            value = value + partner
            step *= 2
    return value


def paired_sum(value, axes):
    first = axes[0]
    count = lax.axis_size(first)
    half = value.shape[0] // 2
    if count < 2 or count & (count - 1) or value.shape[0] % 2:
        total = butterfly_sum(value, axes)
        return total[:half], total[half:], jnp.ones((1, 1), jnp.float32)
    pairs = [(i, i ^ 1) for i in range(count)]
    low = lax.axis_index(first) % 2 == 0
    top, bottom = value[:half], value[half:]
    keep = jnp.where(low, top, bottom)
    give = jnp.where(low, bottom, top)
    part = keep + lax.ppermute(give, first, pairs)
    part = butterfly_sum(part, axes, start=2)
    other = lax.ppermute(part, first, pairs)
    return part, other, jnp.where(low, 1.0, 0.0).reshape(1, 1).astype(jnp.float32)


def core_first(mesh):
    names = tuple(mesh.axis_names)
    devices = mesh.devices
    for pos, name in enumerate(names):
        if devices.shape[pos] < 2:
            continue
        at = [0] * devices.ndim
        one = devices[tuple(at)]
        at[pos] = 1
        two = devices[tuple(at)]
        coords = getattr(one, "coords", None)
        if coords is not None and tuple(coords) == tuple(getattr(two, "coords", ())):
            return (name,) + tuple(n for n in names if n != name)
    return names


def flat_permute(block, axis, pairs):
    pixels = block.size // block.shape[-1]
    if pixels % 64 or pixels <= block.shape[-1]:
        return lax.ppermute(block, axis, pairs)
    flat = block.reshape(pixels // 64, 64, block.shape[-1])
    return lax.ppermute(flat, axis, pairs).reshape(block.shape)


def with_halo(cells, axis, dim, width):
    count = lax.axis_size(axis)
    size = cells.shape[dim]
    head = lax.slice_in_dim(cells, 0, width, axis=dim)
    tail = lax.slice_in_dim(cells, size - width, size, axis=dim)
    before = flat_permute(tail, axis, [(i, i + 1) for i in range(count - 1)])
    after = flat_permute(head, axis, [(i + 1, i) for i in range(count - 1)])
    return jnp.concatenate([before, cells, after], axis=dim)


def pinned(cells):
    return with_layout_constraint(cells, Layout(major_to_minor=tuple(range(cells.ndim))))


def with_ring(cells, width):
    rows_n = lax.axis_size("row")
    cols_n = lax.axis_size("col")
    tile_rows, tile_cols = cells.shape[0], cells.shape[1]
    down = [(i, i + 1) for i in range(rows_n - 1)]
    up = [(i + 1, i) for i in range(rows_n - 1)]
    right = [(i, i + 1) for i in range(cols_n - 1)]
    left = [(i + 1, i) for i in range(cols_n - 1)]
    top = flat_permute(cells[tile_rows - width:], "row", down)
    bottom = flat_permute(cells[:width], "row", up)
    west = lax.ppermute(cells[:, tile_cols - width:], "col", right)
    east = lax.ppermute(cells[:, :width], "col", left)
    rims = jnp.concatenate([top, bottom], axis=0)
    rim_west = lax.ppermute(rims[:, tile_cols - width:], "col", right)
    rim_east = lax.ppermute(rims[:, :width], "col", left)
    return jnp.concatenate(
        [
            jnp.concatenate([rim_west[:width], top, rim_east[:width]], axis=1),
            jnp.concatenate([west, cells, east], axis=1),
            jnp.concatenate([rim_west[width:], bottom, rim_east[width:]], axis=1),
        ],
        axis=0,
    )


def inside_mask(axis, tile, width):
    count = lax.axis_size(axis)
    start = lax.axis_index(axis) * tile - width
    index = start + jnp.arange(tile + 2 * width, dtype=jnp.int32)
    return (index >= 0) & (index < count * tile)


def sweep(field, source, keep):
    diff_col = field[:-1, 1:] - field[:-1, :-1]
    diff_row = field[1:, :-1] - field[:-1, :-1]
    energy_sum = jnp.sum(diff_col * diff_col + diff_row * diff_row, axis=-1, keepdims=True)
    weight = 1.0 / jnp.sqrt(1.0 + energy_sum / field.shape[-1])
    centre = field[1:-1, 1:-1]
    col_here = weight[1:, 1:] * (field[1:-1, 2:] - centre)
    col_left = weight[1:, :-1] * (centre - field[1:-1, :-2])
    row_here = weight[1:, 1:] * (field[2:, 1:-1] - centre)
    row_up = weight[:-1, 1:] * (centre - field[:-2, 1:-1])
    spread = col_here - col_left + row_here - row_up
    new = centre + tau_step * spread + tau_step * fidelity * (source - centre)
    return jnp.where(keep, new, 0.0)


def cholesky_qr(block):
    size = block.shape[1]
    inner = lax.dot_general(
        block, block, (((0,), (0,)), ((), ())),
        precision=lax.Precision.HIGHEST, preferred_element_type=jnp.float32,
    )
    sub = lax.broadcasted_iota(jnp.int32, (size, size), 0)
    lane = lax.broadcasted_iota(jnp.int32, (size, size), 1)
    upper = jnp.zeros((size, size), jnp.float32)
    inverse = jnp.zeros((size, size), jnp.float32)
    rest = inner
    for j in range(size):
        col = rest[:, j:j + 1]
        row = rest[j:j + 1, :]
        pivot = jnp.sqrt(rest[j:j + 1, j:j + 1])
        col = jnp.where(sub[:, :1] >= j, col / pivot, 0.0)
        row = jnp.where(lane[:1] >= j, row / pivot, 0.0)
        upper = upper + jnp.where(sub == j, row, 0.0)
        rest = rest - col * row
        coef = upper[:, j:j + 1]
        diag = upper[j:j + 1, j:j + 1]
        acc = jnp.sum(jnp.where(sub[:, :1] < j, coef, 0.0) * inverse, axis=0, keepdims=True)
        unit = jnp.where(lane[:1] == j, 1.0, 0.0)
        inverse = inverse + jnp.where(sub == j, (unit - acc) / diag, 0.0)
    return lax.dot_general(
        block, inverse, (((1,), (1,)), ((), ())),
        precision=lax.Precision.HIGHEST, preferred_element_type=jnp.float32,
    )


def subspace_kernel(mine_ref, theirs_ref, low_ref, basis_ref, out_ref):
    mine = mine_ref[...]
    theirs = theirs_ref[...]
    if mine.shape == theirs.shape:
        low = low_ref[...] > 0.5
        gram = jnp.concatenate([jnp.where(low, mine, theirs), jnp.where(low, theirs, mine)], axis=0)
    else:
        gram = jnp.concatenate([mine, theirs], axis=0)
    basis = basis_ref[...]
    for turn in range(SUBIT):
        product = jnp.dot(
            gram, basis,
            precision=lax.Precision.HIGHEST, preferred_element_type=jnp.float32,
        )
        basis = cholesky_qr(cholesky_qr(product))
    out_ref[...] = basis


def subspace_step(halves, basis):
    mine, theirs, low = halves
    bands = mine.shape[0] + theirs.shape[0]
    return pl.pallas_call(
        subspace_kernel,
        out_shape=jax.ShapeDtypeStruct(basis.shape, jnp.float32),
        cost_estimate=pl.CostEstimate(
            flops=SUBIT * (2 * bands * bands * basis.shape[1] + 8 * basis.size * basis.shape[1]),
            transcendentals=SUBIT * 2 * basis.shape[1],
            bytes_accessed=4 * (bands * bands + 2 * basis.size),
        ),
    )(mine, theirs, low, basis)


def orthonormal(block):
    inner = jnp.dot(block.T, block, precision=lax.Precision.HIGHEST)
    lower = jnp.linalg.cholesky(inner)
    return lax.linalg.triangular_solve(lower, block, left_side=False, lower=True, transpose_a=True)


def shards(order, image, start_basis):
    band_count, tile_rows, tile_cols = image.shape
    width = SWEEPS
    cells = pinned(jnp.transpose(image, (1, 2, 0)))
    ext = with_ring(cells, width)
    row_in = inside_mask("row", tile_rows, width)
    col_in = inside_mask("col", tile_cols, width)
    field = ext
    for sweep_no in range(SWEEPS):
        left = width - sweep_no - 1
        lo = sweep_no + 1
        nr = tile_rows + 2 * left
        nc = tile_cols + 2 * left
        source = ext[lo:lo + nr, lo:lo + nc]
        keep = (row_in[lo:lo + nr, None] & col_in[None, lo:lo + nc])[:, :, None]
        field = pinned(sweep(field, source, keep))
    flat_cells = field.reshape(tile_rows * tile_cols, band_count)
    smoothed = jnp.transpose(field, (2, 0, 1))
    local_gram = lax.dot_general(
        flat_cells,
        flat_cells,
        (((0,), (0,)), ((), ())),
        precision=lax.Precision.HIGHEST,
        preferred_element_type=jnp.float32,
    )
    gram_halves = paired_sum(local_gram, order)
    basis_now = start_basis
    basis_now = subspace_step(gram_halves, basis_now)
    coeffs = jnp.dot(flat_cells, basis_now, precision=lax.Precision.HIGH)
    lowrank = lax.dot_general(
        basis_now,
        coeffs,
        (((1,), (1,)), ((), ())),
        precision=lax.Precision.HIGH,
    )
    return (smoothed, lowrank.reshape(band_count, tile_rows, tile_cols))


def solution(mesh):
    in_specs = (P(None, "row", "col"), P())
    out_specs = (P(None, "row", "col"), P(None, "row", "col"))
    body = functools.partial(shards, core_first(mesh))
    return jax.shard_map(body, mesh=mesh, in_specs=in_specs, out_specs=out_specs, check_vma=False)
```

```python
import functools

import jax
import jax.numpy as jnp
from jax import lax
from jax.sharding import PartitionSpec as P
from jax.experimental import pallas as pl
from jax.experimental.layout import Layout, with_layout_constraint
from jax.experimental.pallas import tpu as pltpu

SWEEPS = 4
SUBIT = 2


tau_step = 0.22
fidelity = 0.1


def butterfly_sum(value, axes, start=1):
    for axis in axes:
        count = lax.axis_size(axis)
        if count & (count - 1):
            value = lax.psum(value, axis)
            continue
        step = start if axis == axes[0] else 1
        while step < count:
            partner = lax.ppermute(value, axis, [(i, i ^ step) for i in range(count)])
            value = value + partner
            step *= 2
    return value


def paired_sum(value, axes):
    first = axes[0]
    count = lax.axis_size(first)
    half = value.shape[0] // 2
    if count < 2 or count & (count - 1) or value.shape[0] % 2:
        total = butterfly_sum(value, axes)
        return total[:half], total[half:], jnp.ones((1, 1), jnp.float32)
    pairs = [(i, i ^ 1) for i in range(count)]
    low = lax.axis_index(first) % 2 == 0
    top, bottom = value[:half], value[half:]
    keep = jnp.where(low, top, bottom)
    give = jnp.where(low, bottom, top)
    part = keep + lax.ppermute(give, first, pairs)
    part = butterfly_sum(part, axes, start=2)
    other = lax.ppermute(part, first, pairs)
    return part, other, jnp.where(low, 1.0, 0.0).reshape(1, 1).astype(jnp.float32)


def core_first(mesh):
    names = tuple(mesh.axis_names)
    devices = mesh.devices
    for pos, name in enumerate(names):
        if devices.shape[pos] < 2:
            continue
        at = [0] * devices.ndim
        one = devices[tuple(at)]
        at[pos] = 1
        two = devices[tuple(at)]
        coords = getattr(one, "coords", None)
        if coords is not None and tuple(coords) == tuple(getattr(two, "coords", ())):
            return (name,) + tuple(n for n in names if n != name)
    return names


def flat_permute(block, axis, pairs):
    pixels = block.size // block.shape[-1]
    if pixels % 64 or pixels <= block.shape[-1]:
        return lax.ppermute(block, axis, pairs)
    flat = block.reshape(pixels // 64, 64, block.shape[-1])
    return lax.ppermute(flat, axis, pairs).reshape(block.shape)


def with_halo(cells, axis, dim, width):
    count = lax.axis_size(axis)
    size = cells.shape[dim]
    head = lax.slice_in_dim(cells, 0, width, axis=dim)
    tail = lax.slice_in_dim(cells, size - width, size, axis=dim)
    before = flat_permute(tail, axis, [(i, i + 1) for i in range(count - 1)])
    after = flat_permute(head, axis, [(i + 1, i) for i in range(count - 1)])
    return jnp.concatenate([before, cells, after], axis=dim)


def pinned(cells):
    return with_layout_constraint(cells, Layout(major_to_minor=tuple(range(cells.ndim))))


def with_ring(cells, width):
    rows_n = lax.axis_size("row")
    cols_n = lax.axis_size("col")
    tile_rows, tile_cols = cells.shape[0], cells.shape[1]
    down = [(i, i + 1) for i in range(rows_n - 1)]
    up = [(i + 1, i) for i in range(rows_n - 1)]
    right = [(i, i + 1) for i in range(cols_n - 1)]
    left = [(i + 1, i) for i in range(cols_n - 1)]
    top = flat_permute(cells[tile_rows - width:], "row", down)
    bottom = flat_permute(cells[:width], "row", up)
    west = lax.ppermute(cells[:, tile_cols - width:], "col", right)
    east = lax.ppermute(cells[:, :width], "col", left)
    rims = jnp.concatenate([top, bottom], axis=0)
    rim_west = lax.ppermute(rims[:, tile_cols - width:], "col", right)
    rim_east = lax.ppermute(rims[:, :width], "col", left)
    return jnp.concatenate(
        [
            jnp.concatenate([rim_west[:width], top, rim_east[:width]], axis=1),
            jnp.concatenate([west, cells, east], axis=1),
            jnp.concatenate([rim_west[width:], bottom, rim_east[width:]], axis=1),
        ],
        axis=0,
    )


def inside_mask(axis, tile, width):
    count = lax.axis_size(axis)
    start = lax.axis_index(axis) * tile - width
    index = start + jnp.arange(tile + 2 * width, dtype=jnp.int32)
    return (index >= 0) & (index < count * tile)


def sweep(field, source, keep):
    diff_col = field[:-1, 1:] - field[:-1, :-1]
    diff_row = field[1:, :-1] - field[:-1, :-1]
    energy_sum = jnp.sum(diff_col * diff_col + diff_row * diff_row, axis=-1, keepdims=True)
    weight = 1.0 / jnp.sqrt(1.0 + energy_sum / field.shape[-1])
    centre = field[1:-1, 1:-1]
    col_here = weight[1:, 1:] * (field[1:-1, 2:] - centre)
    col_left = weight[1:, :-1] * (centre - field[1:-1, :-2])
    row_here = weight[1:, 1:] * (field[2:, 1:-1] - centre)
    row_up = weight[:-1, 1:] * (centre - field[:-2, 1:-1])
    spread = col_here - col_left + row_here - row_up
    new = centre + tau_step * spread + tau_step * fidelity * (source - centre)
    return new if keep is None else jnp.where(keep, new, 0.0)


def cholesky_qr(block):
    size = block.shape[1]
    inner = lax.dot_general(
        block, block, (((0,), (0,)), ((), ())),
        precision=lax.Precision.HIGHEST, preferred_element_type=jnp.float32,
    )
    sub = lax.broadcasted_iota(jnp.int32, (size, size), 0)
    lane = lax.broadcasted_iota(jnp.int32, (size, size), 1)
    upper = jnp.zeros((size, size), jnp.float32)
    inverse = jnp.zeros((size, size), jnp.float32)
    rest = inner
    for j in range(size):
        col = rest[:, j:j + 1]
        row = rest[j:j + 1, :]
        pivot = jnp.sqrt(rest[j:j + 1, j:j + 1])
        col = jnp.where(sub[:, :1] >= j, col / pivot, 0.0)
        row = jnp.where(lane[:1] >= j, row / pivot, 0.0)
        upper = upper + jnp.where(sub == j, row, 0.0)
        rest = rest - col * row
        coef = upper[:, j:j + 1]
        diag = upper[j:j + 1, j:j + 1]
        acc = jnp.sum(jnp.where(sub[:, :1] < j, coef, 0.0) * inverse, axis=0, keepdims=True)
        unit = jnp.where(lane[:1] == j, 1.0, 0.0)
        inverse = inverse + jnp.where(sub == j, (unit - acc) / diag, 0.0)
    return lax.dot_general(
        block, inverse, (((1,), (1,)), ((), ())),
        precision=lax.Precision.HIGHEST, preferred_element_type=jnp.float32,
    )


def subspace_kernel(mine_ref, theirs_ref, low_ref, basis_ref, out_ref):
    mine = mine_ref[...]
    theirs = theirs_ref[...]
    if mine.shape == theirs.shape:
        low = low_ref[...] > 0.5
        gram = jnp.concatenate([jnp.where(low, mine, theirs), jnp.where(low, theirs, mine)], axis=0)
    else:
        gram = jnp.concatenate([mine, theirs], axis=0)
    basis = basis_ref[...]
    for turn in range(SUBIT):
        product = jnp.dot(
            gram, basis,
            precision=lax.Precision.HIGHEST, preferred_element_type=jnp.float32,
        )
        basis = cholesky_qr(cholesky_qr(product))
    out_ref[...] = basis


def subspace_step(halves, basis):
    mine, theirs, low = halves
    bands = mine.shape[0] + theirs.shape[0]
    return pl.pallas_call(
        subspace_kernel,
        out_shape=jax.ShapeDtypeStruct(basis.shape, jnp.float32),
        cost_estimate=pl.CostEstimate(
            flops=SUBIT * (2 * bands * bands * basis.shape[1] + 8 * basis.size * basis.shape[1]),
            transcendentals=SUBIT * 2 * basis.shape[1],
            bytes_accessed=4 * (bands * bands + 2 * basis.size),
        ),
    )(mine, theirs, low, basis)


def orthonormal(block):
    inner = jnp.dot(block.T, block, precision=lax.Precision.HIGHEST)
    lower = jnp.linalg.cholesky(inner)
    return lax.linalg.triangular_solve(lower, block, left_side=False, lower=True, transpose_a=True)


def shards(order, image, start_basis):
    band_count, tile_rows, tile_cols = image.shape
    width = SWEEPS
    cells = pinned(jnp.transpose(image, (1, 2, 0)))
    ext = with_ring(cells, width)
    row_in = inside_mask("row", tile_rows, width)
    col_in = inside_mask("col", tile_cols, width)
    field = ext
    for sweep_no in range(SWEEPS):
        left = width - sweep_no - 1
        lo = sweep_no + 1
        nr = tile_rows + 2 * left
        nc = tile_cols + 2 * left
        if left == 0:
            field = pinned(sweep(field, cells, None))
            continue
        source = ext[lo:lo + nr, lo:lo + nc]
        keep = (row_in[lo:lo + nr, None] & col_in[None, lo:lo + nc])[:, :, None]
        field = pinned(sweep(field, source, keep))
    flat_cells = field.reshape(tile_rows * tile_cols, band_count)
    smoothed = jnp.transpose(field, (2, 0, 1))
    local_gram = lax.dot_general(
        flat_cells,
        flat_cells,
        (((0,), (0,)), ((), ())),
        precision=lax.Precision.HIGHEST,
        preferred_element_type=jnp.float32,
    )
    gram_halves = paired_sum(local_gram, order)
    basis_now = start_basis
    basis_now = subspace_step(gram_halves, basis_now)
    coeffs = jnp.dot(flat_cells, basis_now, precision=lax.Precision.HIGH)
    lowrank = lax.dot_general(
        basis_now,
        coeffs,
        (((1,), (1,)), ((), ())),
        precision=lax.Precision.HIGH,
    )
    return (smoothed, lowrank.reshape(band_count, tile_rows, tile_cols))


def solution(mesh):
    in_specs = (P(None, "row", "col"), P())
    out_specs = (P(None, "row", "col"), P(None, "row", "col"))
    body = functools.partial(shards, core_first(mesh))
    return jax.shard_map(body, mesh=mesh, in_specs=in_specs, out_specs=out_specs, check_vma=False)
```

```python
import functools

import jax
import jax.numpy as jnp
from jax import lax
from jax.sharding import PartitionSpec as P
from jax.experimental import pallas as pl
from jax.experimental.layout import Layout, with_layout_constraint
from jax.experimental.pallas import tpu as pltpu

SWEEPS = 4
SUBIT = 2


tau_step = 0.22
fidelity = 0.1


def butterfly_sum(value, axes, start=1):
    for axis in axes:
        count = lax.axis_size(axis)
        if count & (count - 1):
            value = lax.psum(value, axis)
            continue
        step = start if axis == axes[0] else 1
        while step < count:
            partner = lax.ppermute(value, axis, [(i, i ^ step) for i in range(count)])
            value = value + partner
            step *= 2
    return value


def paired_sum(value, axes):
    first = axes[0]
    count = lax.axis_size(first)
    half = value.shape[0] // 2
    if count < 2 or count & (count - 1) or value.shape[0] % 2:
        total = butterfly_sum(value, axes)
        return total[:half], total[half:], jnp.ones((1, 1), jnp.float32)
    pairs = [(i, i ^ 1) for i in range(count)]
    low = lax.axis_index(first) % 2 == 0
    top, bottom = value[:half], value[half:]
    keep = jnp.where(low, top, bottom)
    give = jnp.where(low, bottom, top)
    part = keep + lax.ppermute(give, first, pairs)
    part = butterfly_sum(part, axes, start=2)
    other = lax.ppermute(part, first, pairs)
    return part, other, jnp.where(low, 1.0, 0.0).reshape(1, 1).astype(jnp.float32)


def core_first(mesh):
    names = tuple(mesh.axis_names)
    devices = mesh.devices
    for pos, name in enumerate(names):
        if devices.shape[pos] < 2:
            continue
        at = [0] * devices.ndim
        one = devices[tuple(at)]
        at[pos] = 1
        two = devices[tuple(at)]
        coords = getattr(one, "coords", None)
        if coords is not None and tuple(coords) == tuple(getattr(two, "coords", ())):
            return (name,) + tuple(n for n in names if n != name)
    return names


def flat_permute(block, axis, pairs):
    pixels = block.size // block.shape[-1]
    if pixels % 64 or pixels <= block.shape[-1]:
        return lax.ppermute(block, axis, pairs)
    flat = block.reshape(pixels // 64, 64, block.shape[-1])
    return lax.ppermute(flat, axis, pairs).reshape(block.shape)


def with_halo(cells, axis, dim, width):
    count = lax.axis_size(axis)
    size = cells.shape[dim]
    head = lax.slice_in_dim(cells, 0, width, axis=dim)
    tail = lax.slice_in_dim(cells, size - width, size, axis=dim)
    before = flat_permute(tail, axis, [(i, i + 1) for i in range(count - 1)])
    after = flat_permute(head, axis, [(i + 1, i) for i in range(count - 1)])
    return jnp.concatenate([before, cells, after], axis=dim)


def pinned(cells):
    return with_layout_constraint(cells, Layout(major_to_minor=tuple(range(cells.ndim))))


def with_ring(cells, width):
    rows_n = lax.axis_size("row")
    cols_n = lax.axis_size("col")
    tile_rows, tile_cols = cells.shape[0], cells.shape[1]
    down = [(i, i + 1) for i in range(rows_n - 1)]
    up = [(i + 1, i) for i in range(rows_n - 1)]
    right = [(i, i + 1) for i in range(cols_n - 1)]
    left = [(i + 1, i) for i in range(cols_n - 1)]
    top = flat_permute(cells[tile_rows - width:], "row", down)
    bottom = flat_permute(cells[:width], "row", up)
    west = lax.ppermute(cells[:, tile_cols - width:], "col", right)
    east = lax.ppermute(cells[:, :width], "col", left)
    rims = jnp.concatenate([top, bottom], axis=0)
    rim_west = lax.ppermute(rims[:, tile_cols - width:], "col", right)
    rim_east = lax.ppermute(rims[:, :width], "col", left)
    return jnp.concatenate(
        [
            jnp.concatenate([rim_west[:width], top, rim_east[:width]], axis=1),
            jnp.concatenate([west, cells, east], axis=1),
            jnp.concatenate([rim_west[width:], bottom, rim_east[width:]], axis=1),
        ],
        axis=0,
    )


def inside_mask(axis, tile, width):
    count = lax.axis_size(axis)
    start = lax.axis_index(axis) * tile - width
    index = start + jnp.arange(tile + 2 * width, dtype=jnp.int32)
    return (index >= 0) & (index < count * tile)


def sweep(field, source, keep):
    diff_col = field[:-1, 1:] - field[:-1, :-1]
    diff_row = field[1:, :-1] - field[:-1, :-1]
    energy_sum = jnp.sum(diff_col * diff_col + diff_row * diff_row, axis=-1, keepdims=True)
    weight = 1.0 / jnp.sqrt(1.0 + energy_sum / field.shape[-1])
    centre = field[1:-1, 1:-1]
    col_here = weight[1:, 1:] * (field[1:-1, 2:] - centre)
    col_left = weight[1:, :-1] * (centre - field[1:-1, :-2])
    row_here = weight[1:, 1:] * (field[2:, 1:-1] - centre)
    row_up = weight[:-1, 1:] * (centre - field[:-2, 1:-1])
    spread = col_here - col_left + row_here - row_up
    new = centre + tau_step * spread + tau_step * fidelity * (source - centre)
    return jnp.where(keep, new, 0.0)


def cholesky_qr(block):
    size = block.shape[1]
    inner = lax.dot_general(
        block, block, (((0,), (0,)), ((), ())),
        precision=lax.Precision.HIGHEST, preferred_element_type=jnp.float32,
    )
    sub = lax.broadcasted_iota(jnp.int32, (size, size), 0)
    lane = lax.broadcasted_iota(jnp.int32, (size, size), 1)
    upper = jnp.zeros((size, size), jnp.float32)
    inverse = jnp.zeros((size, size), jnp.float32)
    rest = inner
    for j in range(size):
        col = rest[:, j:j + 1]
        row = rest[j:j + 1, :]
        scale = 1.0 / jnp.sqrt(rest[j:j + 1, j:j + 1])
        col = jnp.where(sub[:, :1] >= j, col * scale, 0.0)
        row = jnp.where(lane[:1] >= j, row * scale, 0.0)
        upper = upper + jnp.where(sub == j, row, 0.0)
        rest = rest - col * row
        coef = upper[:, j:j + 1]
        acc = jnp.sum(jnp.where(sub[:, :1] < j, coef, 0.0) * inverse, axis=0, keepdims=True)
        unit = jnp.where(lane[:1] == j, 1.0, 0.0)
        inverse = inverse + jnp.where(sub == j, (unit - acc) * scale, 0.0)
    return lax.dot_general(
        block, inverse, (((1,), (1,)), ((), ())),
        precision=lax.Precision.HIGHEST, preferred_element_type=jnp.float32,
    )


def subspace_kernel(mine_ref, theirs_ref, low_ref, basis_ref, out_ref):
    mine = mine_ref[...]
    theirs = theirs_ref[...]
    if mine.shape == theirs.shape:
        low = low_ref[...] > 0.5
        gram = jnp.concatenate([jnp.where(low, mine, theirs), jnp.where(low, theirs, mine)], axis=0)
    else:
        gram = jnp.concatenate([mine, theirs], axis=0)
    basis = basis_ref[...]
    for turn in range(SUBIT):
        product = jnp.dot(
            gram, basis,
            precision=lax.Precision.HIGHEST, preferred_element_type=jnp.float32,
        )
        basis = cholesky_qr(cholesky_qr(product))
    out_ref[...] = basis


def subspace_step(halves, basis):
    mine, theirs, low = halves
    bands = mine.shape[0] + theirs.shape[0]
    return pl.pallas_call(
        subspace_kernel,
        out_shape=jax.ShapeDtypeStruct(basis.shape, jnp.float32),
        cost_estimate=pl.CostEstimate(
            flops=SUBIT * (2 * bands * bands * basis.shape[1] + 8 * basis.size * basis.shape[1]),
            transcendentals=SUBIT * 2 * basis.shape[1],
            bytes_accessed=4 * (bands * bands + 2 * basis.size),
        ),
    )(mine, theirs, low, basis)


def orthonormal(block):
    inner = jnp.dot(block.T, block, precision=lax.Precision.HIGHEST)
    lower = jnp.linalg.cholesky(inner)
    return lax.linalg.triangular_solve(lower, block, left_side=False, lower=True, transpose_a=True)


def shards(order, image, start_basis):
    band_count, tile_rows, tile_cols = image.shape
    width = SWEEPS
    cells = pinned(jnp.transpose(image, (1, 2, 0)))
    ext = with_ring(cells, width)
    row_in = inside_mask("row", tile_rows, width)
    col_in = inside_mask("col", tile_cols, width)
    field = ext
    for sweep_no in range(SWEEPS):
        left = width - sweep_no - 1
        lo = sweep_no + 1
        nr = tile_rows + 2 * left
        nc = tile_cols + 2 * left
        source = ext[lo:lo + nr, lo:lo + nc]
        keep = (row_in[lo:lo + nr, None] & col_in[None, lo:lo + nc])[:, :, None]
        field = pinned(sweep(field, source, keep))
    flat_cells = field.reshape(tile_rows * tile_cols, band_count)
    smoothed = jnp.transpose(field, (2, 0, 1))
    local_gram = lax.dot_general(
        flat_cells,
        flat_cells,
        (((0,), (0,)), ((), ())),
        precision=lax.Precision.HIGHEST,
        preferred_element_type=jnp.float32,
    )
    gram_halves = paired_sum(local_gram, order)
    basis_now = start_basis
    basis_now = subspace_step(gram_halves, basis_now)
    coeffs = jnp.dot(flat_cells, basis_now, precision=lax.Precision.HIGH)
    lowrank = lax.dot_general(
        basis_now,
        coeffs,
        (((1,), (1,)), ((), ())),
        precision=lax.Precision.HIGH,
    )
    return (smoothed, lowrank.reshape(band_count, tile_rows, tile_cols))


def solution(mesh):
    in_specs = (P(None, "row", "col"), P())
    out_specs = (P(None, "row", "col"), P(None, "row", "col"))
    body = functools.partial(shards, core_first(mesh))
    return jax.shard_map(body, mesh=mesh, in_specs=in_specs, out_specs=out_specs, check_vma=False)
```
